512 devices in a mesh: req: 64 (over x, y, core), head: 8 (over z).
Axes of the slice: x: 4, y: 8, z: 8, core: 2. Of those that a mesh axis runs over, the one named last changes fastest.
Arguments:
- queries: bfloat16 [2, 64, 128, 576], P(None, 'req', 'head'), may hold values from -100 to 100
- prompt_cache: bfloat16 [32768, 576], P('req'), may hold values from -10 to 10
- suffix_cache: bfloat16 [64, 8, 64, 576], P('req'), may hold values from -14 to 14
- new_latent: bfloat16 [2, 64, 576], P(None, 'req'), may hold values from -16 to 16
- suffix_len: int32 [64], P('req'), may hold values from 1 to 512, 16640 in all
- parent: int32 [64], P('req'), may hold values from 0 to 63
- fork_pages: int32 [64, 2], P('req'), may hold values from 0 to 7
Outputs:
- attended: bfloat16 [2, 64, 128, 512], P(None, 'req', 'head')
The draws below stay inside these ranges and needn't reach their ends.
Inputs may be any that keep to these rules, and one draw needn't show every extreme that they name: `suffix_len`: every beam has at least one valid own token.
All inputs are finite; a program needn't handle non-finite values. No bound on the sum of `suffix_len` on one device may be relied on, other than what follows from the above.
Results may differ from the reference program's by a relative error of at most 0.008.
Values may be sent and summed in bfloat16 or wider, within the bound.
No kernel may reach another device: no remote copies, remote signals or barrier semaphores. Data moves between devices by JAX's collectives and lax.ppermute only.
A program may use at most 64 MiB of HBM per device.

```python
import math
import jax
import jax.numpy as jnp
import numpy as np
from jax import lax

DL = 512
DR = 64
HEADS = 128
BEAM_DEV = 1
BEAMS = 64
PROMPT_DEV = 512
PROMPT = 32768
PAGE = 64
SUFFIX_PAGES = 8
FORKS = 2
STEPS = 2
N_REQ = 64


def draw_queries(key, part):
    shape = (STEPS, BEAMS, HEADS, DL + DR)
    values = jnp.clip(jax.random.normal(key, shape, jnp.float32), -6.0, 6.0)
    return values.astype(jnp.bfloat16)


def draw_parent(key, part):
    ranks = jax.random.randint(jax.random.fold_in(key, 11), (BEAMS,), 1, BEAMS + 1)
    order = jax.random.permutation(jax.random.fold_in(key, 13), BEAMS).astype(jnp.int32)
    picked = order[BEAMS // ranks - 1]
    beam_index = jnp.arange(BEAMS, dtype=jnp.int32)
    across = (beam_index + BEAMS // 2) % BEAMS
    forced = (beam_index >= BEAMS // 4) & (beam_index <= BEAMS // 2)
    return jnp.where(forced, across, picked).astype(jnp.int32)


def plant(result, stream_key, smallest, largest):
    shape = result.shape
    spot = [jax.random.randint(jax.random.fold_in(stream_key, axis), (), 0, shape[axis]) for axis in range(len(shape))]
    result = result.at[tuple(spot)].set(smallest)
    longest = shape.index(max(shape))
    spot[longest] = (spot[longest] + 1) % shape[longest]
    return result.at[tuple(spot)].set(largest)


def block_levels(stream_key, extent, cuts, least, top_value):
    loudness = 1.0
    for position, shards_of in cuts:
        draws = jax.random.uniform(jax.random.fold_in(jax.random.fold_in(stream_key, 6), position), (shards_of,), jnp.float32, least / len(cuts), top_value / len(cuts))
        loudness = loudness * jnp.repeat(jnp.exp(draws), extent[position] // shards_of).reshape((-1,) + (1,) * (len(extent) - 1 - position))
    return loudness


def profile(count, total, most, slope):
    weights = [(1 << 20) // math.isqrt(rank ** slope) + 1 for rank in range(2, count + 1)]
    surplus, given = total - most - (count - 1), [1] * (count - 1)
    while surplus > 0:
        free = [i for i in range(count - 1) if given[i] < most]
        pool, remaining = sum([weights[i] for i in free]), surplus
        for i in free:
            extra = min(most - given[i], max(1, remaining * weights[i] // pool), surplus)
            given[i] = given[i] + extra
            surplus = surplus - extra
    return np.array([most] + given)


def uneven(rng, count, total, limit, lean):
    if count == 2:
        one = jax.random.randint(rng, (), max(1, total - limit), min(limit, total - 1) + 1)
        return jnp.stack([one, total - one])
    lengths = jnp.asarray(profile(count, total, limit, lean), jnp.int32)
    pairs = (count - 1) // 2
    donor, receiver = lengths[1:1 + 2 * pairs:2], lengths[2:2 + 2 * pairs:2]
    margin = jnp.minimum(donor - 1, limit - receiver)
    passed = jax.random.randint(jax.random.fold_in(rng, 1), (pairs,), 0, 1 << 20) % (margin + 1)
    lengths = lengths.at[1:1 + 2 * pairs:2].set(donor - passed).at[2:2 + 2 * pairs:2].set(receiver + passed)
    return lengths[jax.random.permutation(jax.random.fold_in(rng, 2), count)]


def scatter_about(stream_key, dims, deviation, limit, split=(), held_as=jnp.bfloat16):
    array = deviation * jax.random.normal(stream_key, dims, jnp.float32)
    if split:
        array = array * block_levels(stream_key, dims, split, -0.22, 0.18)
    return jnp.clip(array, -limit, limit).astype(held_as)


def setup_inputs(seed: int = 0) -> dict:
    streams_of = jax.random.split(jax.random.key(seed), 8)
    return {
        "queries": draw_queries(jax.random.fold_in(streams_of[7], 71), 0),
        "prompt_cache": scatter_about(streams_of[1], (PROMPT, DL + DR), 1.6, 10.0, ((0, 64),)),
        "suffix_cache": scatter_about(streams_of[2], (BEAMS, SUFFIX_PAGES, PAGE, DL + DR), 2.2, 14.0, ((0, 64),)),
        "new_latent": scatter_about(streams_of[3], (STEPS, BEAMS, DL + DR), 3.0, 16.0, ((1, 64),)),
        "suffix_len": uneven(streams_of[4], BEAMS, BEAM_DEV * N_REQ * SUFFIX_PAGES * PAGE // 2 + SUFFIX_PAGES * PAGE // 2, SUFFIX_PAGES * PAGE, 2).astype(jnp.int32),
        "parent": draw_parent(jax.random.fold_in(streams_of[7], 71), 0),
        "fork_pages": plant(jax.random.randint(streams_of[6], (BEAMS, FORKS), 0, SUFFIX_PAGES), jax.random.fold_in(streams_of[6], 1), 0, SUFFIX_PAGES - 1).astype(jnp.int32),
    }


score_scale = 192.0 ** -0.5
neg_large = -1.0e30


def prompt_block(rows, keys):
    scores = jnp.dot(rows, keys.T, preferred_element_type=jnp.float32) * score_scale
    top = jnp.max(scores, axis=-1)
    weights = jnp.exp(scores - top[:, None])
    total = jnp.sum(weights, axis=-1)
    summed = jnp.dot(weights.astype(jnp.bfloat16), keys[:, :DL], preferred_element_type=jnp.float32)
    return top, total, (summed / total[:, None]).astype(jnp.bfloat16)


def masked_partial(queries, keys, valid):
    scores = jnp.einsum("sbhk,btk->sbht", queries.astype(jnp.float32), keys.astype(jnp.float32)) * score_scale
    scores = jnp.where(valid, scores, neg_large)
    top = jnp.max(scores, axis=-1)
    weights = jnp.where(valid, jnp.exp(scores - top[..., None]), 0.0)
    total = jnp.sum(weights, axis=-1)
    rounded = lax.optimization_barrier(weights.astype(jnp.bfloat16)).astype(jnp.float32)
    summed = jnp.einsum("sbht,btd->sbhd", rounded, keys[..., :DL].astype(jnp.float32))
    return top, total, summed


def reference(queries, prompt_cache, suffix_cache, new_latent, suffix_len, parent, fork_pages):
    width = DL + DR
    rows = queries.reshape(-1, width)
    count = rows.shape[0]

    def fold(carry, index):
        peak, denom, numer = carry
        keys = lax.dynamic_slice_in_dim(prompt_cache, (index * PROMPT_DEV).astype(jnp.int32), PROMPT_DEV, 0)
        top, total, out = prompt_block(rows, keys)
        wider = lax.optimization_barrier(out).astype(jnp.float32)
        new_peak = jnp.maximum(peak, top)
        factor = jnp.exp(peak - new_peak)
        weight = total * jnp.exp(top - new_peak)
        return (new_peak, denom * factor + weight, numer * factor[:, None] + weight[:, None] * wider), None

    start = (jnp.full((count,), neg_large, jnp.float32), jnp.zeros((count,), jnp.float32), jnp.zeros((count, DL), jnp.float32))
    (peak_p, denom_p, numer_p), _ = lax.scan(fold, start, jnp.arange(N_REQ, dtype=jnp.int32))
    shape = queries.shape[:3]
    peak_p = peak_p.reshape(shape)
    denom_p = denom_p.reshape(shape)
    numer_p = numer_p.reshape(shape + (DL,))

    tiles = suffix_cache[parent[:, None], fork_pages].reshape(BEAMS, FORKS * PAGE, width)
    positions = (fork_pages[:, :, None] * PAGE + jnp.arange(PAGE, dtype=jnp.int32)[None, None, :]).reshape(BEAMS, -1)
    fork_valid = (positions < suffix_len[parent][:, None])[None, :, None, :]
    top_f, total_f, summed_f = masked_partial(queries, tiles, fork_valid)
    out_f = lax.optimization_barrier((summed_f / jnp.maximum(total_f, 1.0)[..., None]).astype(jnp.bfloat16)).astype(jnp.float32)

    own_keys = jnp.concatenate([suffix_cache.reshape(BEAMS, SUFFIX_PAGES * PAGE, width), jnp.swapaxes(new_latent, 0, 1)], axis=1)
    old_valid = jnp.arange(SUFFIX_PAGES * PAGE, dtype=jnp.int32)[None, :] < suffix_len[:, None]
    new_valid = jnp.arange(STEPS, dtype=jnp.int32)[None, :] <= jnp.arange(STEPS, dtype=jnp.int32)[:, None]
    own_valid = jnp.concatenate([jnp.broadcast_to(old_valid[None], (STEPS, BEAMS, SUFFIX_PAGES * PAGE)), jnp.broadcast_to(new_valid[:, None, :], (STEPS, BEAMS, STEPS))], axis=2)[:, :, None, :]
    top_l, total_l, summed_l = masked_partial(queries, own_keys, own_valid)

    peak = jnp.maximum(jnp.maximum(peak_p, top_f), top_l)
    scale_p = jnp.exp(peak_p - peak)
    weight_f = total_f * jnp.exp(top_f - peak)
    weight_l = jnp.exp(top_l - peak)
    denom = denom_p * scale_p + weight_f + total_l * weight_l
    numer = numer_p * scale_p[..., None] + weight_f[..., None] * out_f + weight_l[..., None] * summed_l
    return (numer / denom[..., None]).astype(jnp.bfloat16)
```

```python
import jax
import jax.numpy as jnp
from jax import lax
from jax.sharding import Mesh
from jax.sharding import PartitionSpec as P

DL = 512
LANES = 128
META_ROWS = 16

score_scale = 192.0 ** (-0.5)
neg_large = -1e30


def masked_softmax(rows, keys, mult):
    scores = jnp.einsum("gqk,tk->gqt", rows, keys, preferred_element_type=jnp.float32) * score_scale
    m = mult[:, None, :]
    valid = m > 0
    top = jnp.max(jnp.where(valid, scores, neg_large), axis=-1)
    weights = jnp.where(valid, jnp.exp(scores - top[..., None]), 0.0)
    total = jnp.sum(weights * m, axis=-1)
    rounded = weights.astype(jnp.bfloat16) * m.astype(jnp.bfloat16)
    summed = jnp.einsum("gqt,td->gqd", rounded, keys[:, :DL], preferred_element_type=jnp.float32)
    return top, total, summed


def own_partial(queries, keys, valid):
    scores = jnp.einsum("shk,tk->sht", queries, keys, preferred_element_type=jnp.float32) * score_scale
    scores = jnp.where(valid, scores, neg_large)
    top = jnp.max(scores, axis=-1)
    weights = jnp.where(valid, jnp.exp(scores - top[..., None]), 0.0)
    total = jnp.sum(weights, axis=-1)
    summed = jnp.einsum(
        "sht,td->shd", weights.astype(jnp.bfloat16), keys[:, :DL], preferred_element_type=jnp.float32
    )
    return top, total, summed


def on_device(queries, prompt_cache, suffix_cache, new_latent, suffix_len, parent, fork_pages):
    steps_n, _, head_dev, width = queries.shape
    pages_n, page_len = suffix_cache.shape[1], suffix_cache.shape[2]
    suffix_n = pages_n * page_len
    prompt_n = prompt_cache.shape[0]
    chips = lax.axis_size("chip")
    chip = lax.axis_index("chip")
    core = lax.axis_index("core")
    my_beam = chip * 2 + core
    partner_beam = chip * 2 + (1 - core)

    q_rows = steps_n * head_dev * width // LANES
    meta = jnp.zeros((META_ROWS, LANES), jnp.bfloat16)
    meta = meta.at[0, 0].set(parent[0].astype(jnp.bfloat16))
    meta = meta.at[0, 1].set(fork_pages[0, 0].astype(jnp.bfloat16))
    meta = meta.at[0, 2].set(fork_pages[0, 1].astype(jnp.bfloat16))
    packed = jnp.concatenate([queries.reshape(q_rows, LANES), meta], axis=0)
    gathered = lax.all_gather(packed, "chip", axis=0, tiled=False)
    rows = gathered[:, :q_rows].reshape(chips, steps_n * head_dev, width)
    meta_all = gathered[:, q_rows, :3].astype(jnp.int32)
    par, fp0, fp1 = meta_all[:, 0], meta_all[:, 1], meta_all[:, 2]

    own_suffix = suffix_cache.reshape(suffix_n, width)
    local_keys = jnp.concatenate([prompt_cache, own_suffix], axis=0)
    partner_keys, partner_len = lax.ppermute((local_keys, suffix_len), "core", [(0, 1), (1, 0)])
    keys = jnp.concatenate([local_keys, partner_keys], axis=0)

    position = jnp.arange(suffix_n, dtype=jnp.int32)
    page = position // page_len

    def fork_count(owner, length):
        hits = (page[None, :] == fp0[:, None]).astype(jnp.float32) + (page[None, :] == fp1[:, None]).astype(
            jnp.float32
        )
        keep = (par == owner)[:, None] & (position < length)[None, :]
        return jnp.where(keep, hits, 0.0)

    ones = jnp.ones((chips, prompt_n), jnp.float32)
    mult = jnp.concatenate(
        [ones, fork_count(my_beam, suffix_len[0]), ones, fork_count(partner_beam, partner_len[0])], axis=1
    )
    top, total, summed = masked_softmax(rows, keys, mult)
    out = (summed / total[..., None]).astype(jnp.bfloat16)

    out_r = lax.all_to_all(out, "chip", 0, 0, tiled=True)
    stats_r = lax.all_to_all(jnp.stack([top, total], axis=-1), "chip", 0, 0, tiled=True)
    top_r = stats_r[..., 0].reshape(chips, steps_n, head_dev)
    total_r = stats_r[..., 1].reshape(chips, steps_n, head_dev)
    out_r = out_r.astype(jnp.float32).reshape(chips, steps_n, head_dev, DL)

    own_keys = jnp.concatenate([own_suffix, new_latent[:, 0, :]], axis=0)
    old_valid = jnp.broadcast_to((position < suffix_len[0])[None, :], (steps_n, suffix_n))
    new_valid = jnp.arange(steps_n, dtype=jnp.int32)[None, :] <= jnp.arange(steps_n, dtype=jnp.int32)[:, None]
    own_valid = jnp.concatenate([old_valid, new_valid], axis=1)[:, None, :]
    top_l, total_l, summed_l = own_partial(queries[:, 0], own_keys, own_valid)

    peak = jnp.maximum(jnp.max(top_r, axis=0), top_l)
    weight_r = total_r * jnp.exp(top_r - peak[None])
    weight_l = jnp.exp(top_l - peak)
    denom = jnp.sum(weight_r, axis=0) + total_l * weight_l
    numer = jnp.sum(weight_r[..., None] * out_r, axis=0) + weight_l[..., None] * summed_l
    result = (numer / denom[..., None]).astype(jnp.bfloat16)
    return result[:, None]


def solution(mesh):
    req_n, head_n = mesh.devices.shape
    devices = mesh.devices.reshape(req_n // 2, 2, head_n)
    split = Mesh(devices, ("chip", "core", "hd"))
    beam = ("chip", "core")
    placed = (
        P(None, beam, "hd", None),
        P(beam, None),
        P(beam, None, None, None),
        P(None, beam, None),
        P(beam),
        P(beam),
        P(beam, None),
    )
    return jax.shard_map(
        on_device,
        mesh=split,
        in_specs=placed,
        out_specs=P(None, beam, "hd", None),
        check_vma=False,
    )
```

```python
import jax
import jax.numpy as jnp
from jax import lax
from jax.sharding import Mesh
from jax.sharding import PartitionSpec as P

DL = 512
LANES = 128
META_ROWS = 16

score_scale = 192.0 ** (-0.5)
neg_large = -1e30


def masked_softmax(rows, keys, mult):
    scores = jnp.einsum("gqk,tk->gqt", rows, keys, preferred_element_type=jnp.float32) * score_scale
    m = mult[:, None, :]
    valid = m > 0
    top = jnp.max(jnp.where(valid, scores, neg_large), axis=-1)
    weights = jnp.where(valid, jnp.exp(scores - top[..., None]), 0.0)
    total = jnp.sum(weights * m, axis=-1)
    rounded = weights.astype(jnp.bfloat16) * m.astype(jnp.bfloat16)
    summed = jnp.einsum("gqt,td->gqd", rounded, keys[:, :DL], preferred_element_type=jnp.float32)
    return top, total, summed


def split3(x):
    hi = lax.reduce_precision(x, exponent_bits=8, mantissa_bits=7)
    rest = x - hi
    mid = lax.reduce_precision(rest, exponent_bits=8, mantissa_bits=7)
    lo = lax.reduce_precision(rest - mid, exponent_bits=8, mantissa_bits=7)
    return [hi.astype(jnp.bfloat16), mid.astype(jnp.bfloat16), lo.astype(jnp.bfloat16)]


def own_partial(queries, keys, valid):
    scores = jnp.einsum("shk,tk->sht", queries, keys, preferred_element_type=jnp.float32) * score_scale
    scores = jnp.where(valid, scores, neg_large)
    top = jnp.max(scores, axis=-1)
    weights = jnp.where(valid, jnp.exp(scores - top[..., None]), 0.0)
    total = jnp.sum(weights, axis=-1)
    summed = jnp.einsum(
        "sht,td->shd", weights.astype(jnp.bfloat16), keys[:, :DL], preferred_element_type=jnp.float32
    )
    return top, total, summed


def on_device(queries, prompt_cache, suffix_cache, new_latent, suffix_len, parent, fork_pages):
    steps_n, _, head_dev, width = queries.shape
    pages_n, page_len = suffix_cache.shape[1], suffix_cache.shape[2]
    suffix_n = pages_n * page_len
    prompt_n = prompt_cache.shape[0]
    chips = lax.axis_size("chip")
    chip = lax.axis_index("chip")
    core = lax.axis_index("core")
    my_beam = chip * 2 + core
    partner_beam = chip * 2 + (1 - core)

    q_rows = steps_n * head_dev * width // LANES
    meta = jnp.zeros((META_ROWS, LANES), jnp.bfloat16)
    meta = meta.at[0, 0].set(parent[0].astype(jnp.bfloat16))
    meta = meta.at[0, 1].set(fork_pages[0, 0].astype(jnp.bfloat16))
    meta = meta.at[0, 2].set(fork_pages[0, 1].astype(jnp.bfloat16))
    packed = jnp.concatenate([queries.reshape(q_rows, LANES), meta], axis=0)
    send = jnp.broadcast_to(packed[None], (chips,) + packed.shape)
    gathered = lax.all_to_all(send, "chip", 0, 0, tiled=True)
    rows = gathered[:, :q_rows].reshape(chips, steps_n * head_dev, width)
    meta_all = gathered[:, q_rows, :3].astype(jnp.int32)
    par, fp0, fp1 = meta_all[:, 0], meta_all[:, 1], meta_all[:, 2]

    own_suffix = suffix_cache.reshape(suffix_n, width)
    local_keys = jnp.concatenate([prompt_cache, own_suffix], axis=0)
    partner_keys, partner_len = lax.ppermute((local_keys, suffix_len), "core", [(0, 1), (1, 0)])
    keys = jnp.concatenate([local_keys, partner_keys], axis=0)

    position = jnp.arange(suffix_n, dtype=jnp.int32)
    page = position // page_len

    def fork_count(owner, length):
        hits = (page[None, :] == fp0[:, None]).astype(jnp.float32) + (page[None, :] == fp1[:, None]).astype(
            jnp.float32
        )
        keep = (par == owner)[:, None] & (position < length)[None, :]
        return jnp.where(keep, hits, 0.0)

    ones = jnp.ones((chips, prompt_n), jnp.float32)
    mult = jnp.concatenate(
        [ones, fork_count(my_beam, suffix_len[0]), ones, fork_count(partner_beam, partner_len[0])], axis=1
    )
    top, total, summed = masked_softmax(rows, keys, mult)
    out = (summed / total[..., None]).astype(jnp.bfloat16)

    out_rows = out.reshape(chips, -1, LANES)
    parts = jnp.stack(split3(top) + split3(total), axis=1).reshape(chips, -1)
    stat_rows = -(-parts.shape[1] // (META_ROWS * LANES)) * META_ROWS
    parts = jnp.pad(parts, ((0, 0), (0, stat_rows * LANES - parts.shape[1])))
    payload = jnp.concatenate([out_rows, parts.reshape(chips, stat_rows, LANES)], axis=1)
    arrived = lax.all_to_all(payload, "chip", 0, 0, tiled=True)
    n_out = out_rows.shape[1]
    out_r = arrived[:, :n_out].astype(jnp.float32).reshape(chips, steps_n, head_dev, DL)
    row_n = steps_n * head_dev
    got = arrived[:, n_out:].reshape(chips, -1)[:, : 6 * row_n].astype(jnp.float32).reshape(chips, 6, row_n)
    top_r = ((got[:, 0] + got[:, 1]) + got[:, 2]).reshape(chips, steps_n, head_dev)
    total_r = ((got[:, 3] + got[:, 4]) + got[:, 5]).reshape(chips, steps_n, head_dev)

    own_keys = jnp.concatenate([own_suffix, new_latent[:, 0, :]], axis=0)
    old_valid = jnp.broadcast_to((position < suffix_len[0])[None, :], (steps_n, suffix_n))
    new_valid = jnp.arange(steps_n, dtype=jnp.int32)[None, :] <= jnp.arange(steps_n, dtype=jnp.int32)[:, None]
    own_valid = jnp.concatenate([old_valid, new_valid], axis=1)[:, None, :]
    top_l, total_l, summed_l = own_partial(queries[:, 0], own_keys, own_valid)

    peak = jnp.maximum(jnp.max(top_r, axis=0), top_l)
    weight_r = total_r * jnp.exp(top_r - peak[None])
    weight_l = jnp.exp(top_l - peak)
    denom = jnp.sum(weight_r, axis=0) + total_l * weight_l
    numer = jnp.sum(weight_r[..., None] * out_r, axis=0) + weight_l[..., None] * summed_l
    result = (numer / denom[..., None]).astype(jnp.bfloat16)
    return result[:, None]


def solution(mesh):
    req_n, head_n = mesh.devices.shape
    devices = mesh.devices.reshape(req_n // 2, 2, head_n)
    split = Mesh(devices, ("chip", "core", "hd"))
    beam = ("chip", "core")
    placed = (
        P(None, beam, "hd", None),
        P(beam, None),
        P(beam, None, None, None),
        P(None, beam, None),
        P(beam),
        P(beam),
        P(beam, None),
    )
    return jax.shard_map(
        on_device,
        mesh=split,
        in_specs=placed,
        out_specs=P(None, beam, "hd", None),
        check_vma=False,
    )
```

```python
import jax
import jax.numpy as jnp
from jax import lax
from jax.sharding import Mesh
from jax.sharding import PartitionSpec as P

DL = 512
LANES = 128
META_ROWS = 16

score_scale = 192.0 ** (-0.5)
neg_large = -1e30


def masked_softmax(rows, keys, mult):
    scores = jnp.einsum("gqk,tk->gqt", rows, keys, preferred_element_type=jnp.float32) * score_scale
    m = mult[:, None, :]
    valid = m > 0
    top = jnp.max(jnp.where(valid, scores, neg_large), axis=-1)
    weights = jnp.where(valid, jnp.exp(scores - top[..., None]), 0.0)
    total = jnp.sum(weights * m, axis=-1)
    rounded = weights.astype(jnp.bfloat16) * m.astype(jnp.bfloat16)
    summed = jnp.einsum("gqt,td->gqd", rounded, keys[:, :DL], preferred_element_type=jnp.float32)
    return top, total, summed


def split3(x):
    hi = lax.reduce_precision(x, exponent_bits=8, mantissa_bits=7)
    rest = x - hi
    mid = lax.reduce_precision(rest, exponent_bits=8, mantissa_bits=7)
    lo = lax.reduce_precision(rest - mid, exponent_bits=8, mantissa_bits=7)
    return [hi.astype(jnp.bfloat16), mid.astype(jnp.bfloat16), lo.astype(jnp.bfloat16)]


def own_partial(queries, keys, valid):
    scores = jnp.einsum("shk,tk->sht", queries, keys, preferred_element_type=jnp.float32) * score_scale
    scores = jnp.where(valid, scores, neg_large)
    top = jnp.max(scores, axis=-1)
    weights = jnp.where(valid, jnp.exp(scores - top[..., None]), 0.0)
    total = jnp.sum(weights, axis=-1)
    summed = jnp.einsum(
        "sht,td->shd", weights.astype(jnp.bfloat16), keys[:, :DL], preferred_element_type=jnp.float32
    )
    return top, total, summed


def on_device(queries, prompt_cache, suffix_cache, new_latent, suffix_len, parent, fork_pages):
    steps_n, _, head_dev, width = queries.shape
    pages_n, page_len = suffix_cache.shape[1], suffix_cache.shape[2]
    suffix_n = pages_n * page_len
    prompt_n = prompt_cache.shape[0]
    chips = lax.axis_size("cx") * lax.axis_size("cy")
    chip = lax.axis_index("cx") * lax.axis_size("cy") + lax.axis_index("cy")
    core = lax.axis_index("core")
    my_beam = chip * 2 + core
    partner_beam = chip * 2 + (1 - core)

    q_rows = steps_n * head_dev * width // LANES
    lane = lax.broadcasted_iota(jnp.int32, (META_ROWS, LANES), 1)
    first = lax.broadcasted_iota(jnp.int32, (META_ROWS, LANES), 0) == 0
    meta = jnp.where(lane == 0, parent[0], jnp.where(lane == 1, fork_pages[0, 0], fork_pages[0, 1]))
    meta = jnp.where(first & (lane < 3), meta, 0).astype(jnp.bfloat16)
    packed = jnp.concatenate([queries.reshape(q_rows, LANES), meta], axis=0)
    along_y = lax.all_to_all(
        jnp.broadcast_to(packed[None], (lax.axis_size("cy"),) + packed.shape), "cy", 0, 0, tiled=True
    )
    gathered = lax.all_to_all(
        jnp.broadcast_to(along_y[None], (lax.axis_size("cx"),) + along_y.shape), "cx", 0, 0, tiled=True
    ).reshape((chips,) + packed.shape)
    rows = gathered[:, :q_rows].reshape(chips, steps_n * head_dev, width)
    meta_all = gathered[:, q_rows, :3].astype(jnp.int32)
    par, fp0, fp1 = meta_all[:, 0], meta_all[:, 1], meta_all[:, 2]

    own_suffix = suffix_cache.reshape(suffix_n, width)
    local_keys = jnp.concatenate([prompt_cache, own_suffix], axis=0)
    partner_keys, partner_len = lax.ppermute((local_keys, suffix_len), "core", [(0, 1), (1, 0)])
    keys = jnp.concatenate([local_keys, partner_keys], axis=0)

    position = jnp.arange(suffix_n, dtype=jnp.int32)
    page = position // page_len

    def fork_count(owner, length):
        hits = (page[None, :] == fp0[:, None]).astype(jnp.float32) + (page[None, :] == fp1[:, None]).astype(
            jnp.float32
        )
        keep = (par == owner)[:, None] & (position < length)[None, :]
        return jnp.where(keep, hits, 0.0)

    ones = jnp.ones((chips, prompt_n), jnp.float32)
    mult = jnp.concatenate(
        [ones, fork_count(my_beam, suffix_len[0]), ones, fork_count(partner_beam, partner_len[0])], axis=1
    )
    top, total, summed = masked_softmax(rows, keys, mult)
    out = (summed / total[..., None]).astype(jnp.bfloat16)

    out_rows = out.reshape(chips, -1, LANES)
    parts = jnp.stack(split3(top) + split3(total), axis=1).reshape(chips, -1)
    stat_rows = -(-parts.shape[1] // (META_ROWS * LANES)) * META_ROWS
    parts = jnp.pad(parts, ((0, 0), (0, stat_rows * LANES - parts.shape[1])))
    payload = jnp.concatenate([out_rows, parts.reshape(chips, stat_rows, LANES)], axis=1)
    arrived = lax.all_to_all(payload, ("cx", "cy"), 0, 0, tiled=True)
    n_out = out_rows.shape[1]
    row_n = steps_n * head_dev
    out_r = arrived[:, :n_out].reshape(chips, row_n, DL)
    got = arrived[:, n_out:].reshape(chips, -1)[:, : 6 * row_n].astype(jnp.float32).reshape(chips, 6, row_n)
    top_r = (got[:, 0] + got[:, 1]) + got[:, 2]
    total_r = (got[:, 3] + got[:, 4]) + got[:, 5]

    own_keys = jnp.concatenate([own_suffix, new_latent[:, 0, :]], axis=0)
    old_valid = jnp.broadcast_to((position < suffix_len[0])[None, :], (steps_n, suffix_n))
    new_valid = jnp.arange(steps_n, dtype=jnp.int32)[None, :] <= jnp.arange(steps_n, dtype=jnp.int32)[:, None]
    own_valid = jnp.concatenate([old_valid, new_valid], axis=1)[:, None, :]
    top_l, total_l, summed_l = own_partial(queries[:, 0], own_keys, own_valid)

    top_l = top_l.reshape(row_n)
    total_l = total_l.reshape(row_n)
    summed_l = summed_l.reshape(row_n, DL)
    peak = jnp.maximum(jnp.max(top_r, axis=0), top_l)
    weight_r = total_r * jnp.exp(top_r - peak[None])
    weight_l = jnp.exp(top_l - peak)
    denom = jnp.sum(weight_r, axis=0) + total_l * weight_l
    numer = jnp.sum(weight_r[..., None] * out_r.astype(jnp.float32), axis=0) + weight_l[:, None] * summed_l
    result = (numer / denom[:, None]).astype(jnp.bfloat16)
    return result.reshape(steps_n, 1, head_dev, DL)


def chip_grid(devices):
    try:
        xs = {d.coords[0] for d in devices.flat}
        ys = {d.coords[1] for d in devices.flat}
        if len(xs) * len(ys) * 2 == devices.shape[0]:
            return len(xs), len(ys)
    except (AttributeError, IndexError, TypeError):
        pass
    return 1, devices.shape[0] // 2


def solution(mesh):
    req_n, head_n = mesh.devices.shape
    x_n, y_n = chip_grid(mesh.devices)
    devices = mesh.devices.reshape(x_n, y_n, 2, head_n)
    split = Mesh(devices, ("cx", "cy", "core", "hd"))
    beam = ("cx", "cy", "core")
    placed = (
        P(None, beam, "hd", None),
        P(beam, None),
        P(beam, None, None, None),
        P(None, beam, None),
        P(beam),
        P(beam),
        P(beam, None),
    )
    return jax.shard_map(
        on_device,
        mesh=split,
        in_specs=placed,
        out_specs=P(None, beam, "hd", None),
        check_vma=False,
    )
```

```python
import functools

import jax
import jax.numpy as jnp
from jax import lax
from jax.experimental import pallas as pl
from jax.experimental.pallas import tpu as pltpu
from jax.sharding import Mesh
from jax.sharding import PartitionSpec as P

DL = 512
LANES = 128
META_ROWS = 16

score_scale = 192.0 ** (-0.5)
neg_large = -1e30
INTERPRET = False
GROUP_BEAMS = 8


def softmax_kernel(q_ref, k_ref, m_ref, out_ref, stat_ref):
    groups, key_n = m_ref.shape
    rows_n = q_ref.shape[0]
    per = rows_n // groups
    scores = lax.dot_general(
        q_ref[...], k_ref[...], (((1,), (1,)), ((), ())), preferred_element_type=jnp.float32
    ) * score_scale
    m = jnp.broadcast_to(m_ref[...][:, None, :], (groups, per, key_n)).reshape(rows_n, key_n)
    valid = m > 0
    top = jnp.max(jnp.where(valid, scores, neg_large), axis=1, keepdims=True)
    weights = jnp.where(valid, jnp.exp(scores - top), 0.0)
    total = jnp.sum(weights * m, axis=1, keepdims=True)
    rounded = weights.astype(jnp.bfloat16) * m.astype(jnp.bfloat16)
    summed = jnp.dot(rounded, k_ref[:, :DL], preferred_element_type=jnp.float32)
    out_ref[...] = (summed / total).astype(out_ref.dtype)
    lane = lax.broadcasted_iota(jnp.int32, stat_ref.shape, 1)
    stat_ref[...] = jnp.where(lane < LANES // 2, top, total)


def fused_softmax(rows, keys, mult):
    rows_n, width = rows.shape
    key_n = keys.shape[0]
    groups = mult.shape[0]
    per = rows_n // groups
    step_rows = GROUP_BEAMS * per
    grid = (groups // GROUP_BEAMS,)
    cost = pl.CostEstimate(
        flops=2 * rows_n * key_n * (width + DL),
        transcendentals=rows_n * key_n,
        bytes_accessed=2 * (rows_n * width + key_n * width + rows_n * DL) + 4 * (groups * key_n + rows_n * LANES),
    )
    out, stat = pl.pallas_call(
        softmax_kernel,
        grid=grid,
        in_specs=[
            pl.BlockSpec((step_rows, width), lambda i: (i, 0)),
            pl.BlockSpec((key_n, width), lambda i: (0, 0)),
            pl.BlockSpec((GROUP_BEAMS, key_n), lambda i: (i, 0)),
        ],
        out_specs=[
            pl.BlockSpec((step_rows, DL), lambda i: (i, 0)),
            pl.BlockSpec((step_rows, LANES), lambda i: (i, 0)),
        ],
        out_shape=[
            jax.ShapeDtypeStruct((rows_n, DL), jnp.bfloat16),
            jax.ShapeDtypeStruct((rows_n, LANES), jnp.float32),
        ],
        compiler_params=pltpu.CompilerParams(vmem_limit_bytes=48 * 1024 * 1024),
        cost_estimate=cost,
        interpret=INTERPRET,
    )(rows, keys, mult)
    return out, stat[:, 0], stat[:, LANES // 2]


def masked_softmax(rows, keys, mult):
    scores = jnp.einsum("gqk,tk->gqt", rows, keys, preferred_element_type=jnp.float32) * score_scale
    m = mult[:, None, :]
    valid = m > 0
    top = jnp.max(jnp.where(valid, scores, neg_large), axis=-1)
    weights = jnp.where(valid, jnp.exp(scores - top[..., None]), 0.0)
    total = jnp.sum(weights * m, axis=-1)
    rounded = weights.astype(jnp.bfloat16) * m.astype(jnp.bfloat16)
    summed = jnp.einsum("gqt,td->gqd", rounded, keys[:, :DL], preferred_element_type=jnp.float32)
    return top, total, summed


def split3(x):
    hi = lax.reduce_precision(x, exponent_bits=8, mantissa_bits=7)
    rest = x - hi
    mid = lax.reduce_precision(rest, exponent_bits=8, mantissa_bits=7)
    lo = lax.reduce_precision(rest - mid, exponent_bits=8, mantissa_bits=7)
    return [hi.astype(jnp.bfloat16), mid.astype(jnp.bfloat16), lo.astype(jnp.bfloat16)]


def own_partial(queries, keys, valid):
    scores = jnp.einsum("shk,tk->sht", queries, keys, preferred_element_type=jnp.float32) * score_scale
    scores = jnp.where(valid, scores, neg_large)
    top = jnp.max(scores, axis=-1)
    weights = jnp.where(valid, jnp.exp(scores - top[..., None]), 0.0)
    total = jnp.sum(weights, axis=-1)
    summed = jnp.einsum(
        "sht,td->shd", weights.astype(jnp.bfloat16), keys[:, :DL], preferred_element_type=jnp.float32
    )
    return top, total, summed


def on_device(queries, prompt_cache, suffix_cache, new_latent, suffix_len, parent, fork_pages):
    steps_n, _, head_dev, width = queries.shape
    pages_n, page_len = suffix_cache.shape[1], suffix_cache.shape[2]
    suffix_n = pages_n * page_len
    prompt_n = prompt_cache.shape[0]
    chips = lax.axis_size("cx") * lax.axis_size("cy")
    chip = lax.axis_index("cx") * lax.axis_size("cy") + lax.axis_index("cy")
    core = lax.axis_index("core")
    my_beam = chip * 2 + core
    partner_beam = chip * 2 + (1 - core)

    q_rows = steps_n * head_dev * width // LANES
    lane = lax.broadcasted_iota(jnp.int32, (META_ROWS, LANES), 1)
    first = lax.broadcasted_iota(jnp.int32, (META_ROWS, LANES), 0) == 0
    meta = jnp.where(lane == 0, parent[0], jnp.where(lane == 1, fork_pages[0, 0], fork_pages[0, 1]))
    meta = jnp.where(first & (lane < 3), meta, 0).astype(jnp.bfloat16)
    packed = jnp.concatenate([queries.reshape(q_rows, LANES), meta], axis=0)
    along_y = lax.all_to_all(
        jnp.broadcast_to(packed[None], (lax.axis_size("cy"),) + packed.shape), "cy", 0, 0, tiled=True
    )
    gathered = lax.all_to_all(
        jnp.broadcast_to(along_y[None], (lax.axis_size("cx"),) + along_y.shape), "cx", 0, 0, tiled=True
    ).reshape((chips,) + packed.shape)
    rows = gathered[:, :q_rows].reshape(chips, steps_n * head_dev, width)
    meta_all = gathered[:, q_rows, :3].astype(jnp.int32)
    par, fp0, fp1 = meta_all[:, 0], meta_all[:, 1], meta_all[:, 2]

    own_suffix = suffix_cache.reshape(suffix_n, width)
    local_keys = jnp.concatenate([prompt_cache, own_suffix], axis=0)
    partner_keys, partner_len = lax.ppermute((local_keys, suffix_len), "core", [(0, 1), (1, 0)])
    keys = jnp.concatenate([local_keys, partner_keys], axis=0)

    position = jnp.arange(suffix_n, dtype=jnp.int32)
    page = position // page_len

    def fork_count(owner, length):
        hits = (page[None, :] == fp0[:, None]).astype(jnp.float32) + (page[None, :] == fp1[:, None]).astype(
            jnp.float32
        )
        keep = (par == owner)[:, None] & (position < length)[None, :]
        return jnp.where(keep, hits, 0.0)

    ones = jnp.ones((chips, prompt_n), jnp.float32)
    mult = jnp.concatenate(
        [ones, fork_count(my_beam, suffix_len[0]), ones, fork_count(partner_beam, partner_len[0])], axis=1
    )
    row_n = steps_n * head_dev
    out, top, total = fused_softmax(rows.reshape(chips * row_n, width), keys, mult)
    out = out.reshape(chips, row_n, DL)
    top = top.reshape(chips, row_n)
    total = total.reshape(chips, row_n)

    out_rows = out.reshape(chips, -1, LANES)
    parts = jnp.stack(split3(top) + split3(total), axis=1).reshape(chips, -1)
    stat_rows = -(-parts.shape[1] // (META_ROWS * LANES)) * META_ROWS
    parts = jnp.pad(parts, ((0, 0), (0, stat_rows * LANES - parts.shape[1])))
    payload = jnp.concatenate([out_rows, parts.reshape(chips, stat_rows, LANES)], axis=1)
    arrived = lax.all_to_all(payload, ("cx", "cy"), 0, 0, tiled=True)
    n_out = out_rows.shape[1]
    out_r = arrived[:, :n_out].reshape(chips, row_n, DL)
    got = arrived[:, n_out:].reshape(chips, -1)[:, : 6 * row_n].astype(jnp.float32).reshape(chips, 6, row_n)
    top_r = (got[:, 0] + got[:, 1]) + got[:, 2]
    total_r = (got[:, 3] + got[:, 4]) + got[:, 5]

    own_keys = jnp.concatenate([own_suffix, new_latent[:, 0, :]], axis=0)
    old_valid = jnp.broadcast_to((position < suffix_len[0])[None, :], (steps_n, suffix_n))
    new_valid = jnp.arange(steps_n, dtype=jnp.int32)[None, :] <= jnp.arange(steps_n, dtype=jnp.int32)[:, None]
    own_valid = jnp.concatenate([old_valid, new_valid], axis=1)[:, None, :]
    top_l, total_l, summed_l = own_partial(queries[:, 0], own_keys, own_valid)

    top_l = top_l.reshape(row_n)
    total_l = total_l.reshape(row_n)
    summed_l = summed_l.reshape(row_n, DL)
    peak = jnp.maximum(jnp.max(top_r, axis=0), top_l)
    weight_r = total_r * jnp.exp(top_r - peak[None])
    weight_l = jnp.exp(top_l - peak)
    denom = jnp.sum(weight_r, axis=0) + total_l * weight_l
    numer = jnp.sum(weight_r[..., None] * out_r.astype(jnp.float32), axis=0) + weight_l[:, None] * summed_l
    result = (numer / denom[:, None]).astype(jnp.bfloat16)
    return result.reshape(steps_n, 1, head_dev, DL)


def chip_grid(devices):
    try:
        xs = {d.coords[0] for d in devices.flat}
        ys = {d.coords[1] for d in devices.flat}
        if len(xs) * len(ys) * 2 == devices.shape[0]:
            return len(xs), len(ys)
    except (AttributeError, IndexError, TypeError):
        pass
    return 1, devices.shape[0] // 2


def solution(mesh):
    req_n, head_n = mesh.devices.shape
    x_n, y_n = chip_grid(mesh.devices)
    devices = mesh.devices.reshape(x_n, y_n, 2, head_n)
    split = Mesh(devices, ("cx", "cy", "core", "hd"))
    beam = ("cx", "cy", "core")
    placed = (
        P(None, beam, "hd", None),
        P(beam, None),
        P(beam, None, None, None),
        P(None, beam, None),
        P(beam),
        P(beam),
        P(beam, None),
    )
    return jax.shard_map(
        on_device,
        mesh=split,
        in_specs=placed,
        out_specs=P(None, beam, "hd", None),
        check_vma=False,
    )
```

```python
import jax
import jax.numpy as jnp
from jax import lax
from jax.sharding import Mesh
from jax.sharding import PartitionSpec as P

DL = 512
LANES = 128
META_ROWS = 16

score_scale = 192.0 ** (-0.5)
neg_large = -1e30


def masked_softmax(rows, keys, mult):
    scores = jnp.einsum("gqk,tk->gqt", rows, keys, preferred_element_type=jnp.float32) * score_scale
    m = mult[:, None, :]
    valid = m > 0
    top = jnp.max(jnp.where(valid, scores, neg_large), axis=-1)
    weights = jnp.where(valid, jnp.exp(scores - top[..., None]), 0.0)
    total = jnp.sum(weights * m, axis=-1)
    rounded = weights.astype(jnp.bfloat16) * m.astype(jnp.bfloat16)
    summed = jnp.einsum("gqt,td->gqd", rounded, keys[:, :DL], preferred_element_type=jnp.float32)
    return top, total, summed


def split3(x):
    hi = lax.reduce_precision(x, exponent_bits=8, mantissa_bits=7)
    rest = x - hi
    mid = lax.reduce_precision(rest, exponent_bits=8, mantissa_bits=7)
    lo = lax.reduce_precision(rest - mid, exponent_bits=8, mantissa_bits=7)
    return [hi.astype(jnp.bfloat16), mid.astype(jnp.bfloat16), lo.astype(jnp.bfloat16)]


def pack_partials(out, top, total):
    n = out.shape[0]
    out_rows = out.reshape(n, -1, LANES)
    parts = jnp.stack(split3(top) + split3(total), axis=1).reshape(n, -1)
    stat_rows = -(-parts.shape[1] // (META_ROWS * LANES)) * META_ROWS
    parts = jnp.pad(parts, ((0, 0), (0, stat_rows * LANES - parts.shape[1])))
    return jnp.concatenate([out_rows, parts.reshape(n, stat_rows, LANES)], axis=1)


def unpack_partials(arrived, row_n):
    n = arrived.shape[0]
    n_out = row_n * DL // LANES
    out = arrived[:, :n_out].reshape(n, row_n, DL).astype(jnp.float32)
    got = arrived[:, n_out:].reshape(n, -1)[:, : 6 * row_n].astype(jnp.float32).reshape(n, 6, row_n)
    top = (got[:, 0] + got[:, 1]) + got[:, 2]
    total = (got[:, 3] + got[:, 4]) + got[:, 5]
    return out, top, total


def own_partial(queries, keys, valid):
    scores = jnp.einsum("shk,tk->sht", queries, keys, preferred_element_type=jnp.float32) * score_scale
    scores = jnp.where(valid, scores, neg_large)
    top = jnp.max(scores, axis=-1)
    weights = jnp.where(valid, jnp.exp(scores - top[..., None]), 0.0)
    total = jnp.sum(weights, axis=-1)
    summed = jnp.einsum(
        "sht,td->shd", weights.astype(jnp.bfloat16), keys[:, :DL], preferred_element_type=jnp.float32
    )
    return top, total, summed


def on_device(queries, prompt_cache, suffix_cache, new_latent, suffix_len, parent, fork_pages):
    steps_n, _, head_dev, width = queries.shape
    pages_n, page_len = suffix_cache.shape[1], suffix_cache.shape[2]
    suffix_n = pages_n * page_len
    prompt_n = prompt_cache.shape[0]
    chips = lax.axis_size("cx") * lax.axis_size("cy")
    chip = lax.axis_index("cx") * lax.axis_size("cy") + lax.axis_index("cy")
    core = lax.axis_index("core")
    my_beam = chip * 2 + core
    partner_beam = chip * 2 + (1 - core)

    q_rows = steps_n * head_dev * width // LANES
    lane = lax.broadcasted_iota(jnp.int32, (META_ROWS, LANES), 1)
    first = lax.broadcasted_iota(jnp.int32, (META_ROWS, LANES), 0) == 0
    meta = jnp.where(lane == 0, parent[0], jnp.where(lane == 1, fork_pages[0, 0], fork_pages[0, 1]))
    meta = jnp.where(first & (lane < 3), meta, 0).astype(jnp.bfloat16)
    packed = jnp.concatenate([queries.reshape(q_rows, LANES), meta], axis=0)
    along_y = lax.all_to_all(
        jnp.broadcast_to(packed[None], (lax.axis_size("cy"),) + packed.shape), "cy", 0, 0, tiled=True
    )
    gathered = lax.all_to_all(
        jnp.broadcast_to(along_y[None], (lax.axis_size("cx"),) + along_y.shape), "cx", 0, 0, tiled=True
    ).reshape((chips,) + packed.shape)
    rows = gathered[:, :q_rows].reshape(chips, steps_n * head_dev, width)
    meta_all = gathered[:, q_rows, :3].astype(jnp.int32)
    par, fp0, fp1 = meta_all[:, 0], meta_all[:, 1], meta_all[:, 2]

    own_suffix = suffix_cache.reshape(suffix_n, width)
    local_keys = jnp.concatenate([prompt_cache, own_suffix], axis=0)
    partner_keys, partner_len = lax.ppermute((local_keys, suffix_len), "core", [(0, 1), (1, 0)])
    keys = jnp.concatenate([local_keys, partner_keys], axis=0)

    position = jnp.arange(suffix_n, dtype=jnp.int32)
    page = position // page_len

    def fork_count(owner, length):
        hits = (page[None, :] == fp0[:, None]).astype(jnp.float32) + (page[None, :] == fp1[:, None]).astype(
            jnp.float32
        )
        keep = (par == owner)[:, None] & (position < length)[None, :]
        return jnp.where(keep, hits, 0.0)

    ones = jnp.ones((chips, prompt_n), jnp.float32)
    mult = jnp.concatenate(
        [ones, fork_count(my_beam, suffix_len[0]), ones, fork_count(partner_beam, partner_len[0])], axis=1
    )
    top, total, summed = masked_softmax(rows, keys, mult)
    out = (summed / total[..., None]).astype(jnp.bfloat16)

    x_n, y_n = lax.axis_size("cx"), lax.axis_size("cy")
    row_n = steps_n * head_dev
    payload = pack_partials(out, top, total)
    arrived = lax.all_to_all(payload.reshape(x_n, -1, LANES), "cx", 0, 0, tiled=True)
    out_x, top_x, total_x = unpack_partials(arrived.reshape(x_n * y_n, -1, LANES), row_n)
    out_x = out_x.reshape(x_n, y_n, row_n, DL)
    top_x = top_x.reshape(x_n, y_n, row_n)
    total_x = total_x.reshape(x_n, y_n, row_n)
    top_m = jnp.max(top_x, axis=0)
    weight_x = total_x * jnp.exp(top_x - top_m[None])
    total_m = jnp.sum(weight_x, axis=0)
    out_m = jnp.sum(weight_x[..., None] * out_x, axis=0) / total_m[..., None]
    arrived = lax.all_to_all(pack_partials(out_m.astype(jnp.bfloat16), top_m, total_m), "cy", 0, 0, tiled=True)
    out_r, top_r, total_r = unpack_partials(arrived, row_n)

    own_keys = jnp.concatenate([own_suffix, new_latent[:, 0, :]], axis=0)
    old_valid = jnp.broadcast_to((position < suffix_len[0])[None, :], (steps_n, suffix_n))
    new_valid = jnp.arange(steps_n, dtype=jnp.int32)[None, :] <= jnp.arange(steps_n, dtype=jnp.int32)[:, None]
    own_valid = jnp.concatenate([old_valid, new_valid], axis=1)[:, None, :]
    top_l, total_l, summed_l = own_partial(queries[:, 0], own_keys, own_valid)

    top_l = top_l.reshape(row_n)
    total_l = total_l.reshape(row_n)
    summed_l = summed_l.reshape(row_n, DL)
    peak = jnp.maximum(jnp.max(top_r, axis=0), top_l)
    weight_r = total_r * jnp.exp(top_r - peak[None])
    weight_l = jnp.exp(top_l - peak)
    denom = jnp.sum(weight_r, axis=0) + total_l * weight_l
    numer = jnp.sum(weight_r[..., None] * out_r, axis=0) + weight_l[:, None] * summed_l
    result = (numer / denom[:, None]).astype(jnp.bfloat16)
    return result.reshape(steps_n, 1, head_dev, DL)


def chip_grid(devices):
    try:
        xs = {d.coords[0] for d in devices.flat}
        ys = {d.coords[1] for d in devices.flat}
        if len(xs) * len(ys) * 2 == devices.shape[0]:
            return len(xs), len(ys)
    except (AttributeError, IndexError, TypeError):
        pass
    return 1, devices.shape[0] // 2


def solution(mesh):
    req_n, head_n = mesh.devices.shape
    x_n, y_n = chip_grid(mesh.devices)
    devices = mesh.devices.reshape(x_n, y_n, 2, head_n)
    split = Mesh(devices, ("cx", "cy", "core", "hd"))
    beam = ("cx", "cy", "core")
    placed = (
        P(None, beam, "hd", None),
        P(beam, None),
        P(beam, None, None, None),
        P(None, beam, None),
        P(beam),
        P(beam),
        P(beam, None),
    )
    return jax.shard_map(
        on_device,
        mesh=split,
        in_specs=placed,
        out_specs=P(None, beam, "hd", None),
        check_vma=False,
    )
```

```python
import jax
import jax.numpy as jnp
from jax import lax
from jax.sharding import Mesh
from jax.sharding import PartitionSpec as P

DL = 512
LANES = 128
META_ROWS = 16

score_scale = 192.0 ** (-0.5)
neg_large = -1e30


def masked_softmax(rows, keys, mult):
    scores = jnp.einsum("gqk,tk->gqt", rows, keys, preferred_element_type=jnp.float32) * score_scale
    m = mult[:, None, :]
    valid = m > 0
    top = jnp.max(jnp.where(valid, scores, neg_large), axis=-1)
    weights = jnp.where(valid, jnp.exp(scores - top[..., None]), 0.0)
    total = jnp.sum(weights * m, axis=-1)
    rounded = weights.astype(jnp.bfloat16) * m.astype(jnp.bfloat16)
    summed = jnp.einsum("gqt,td->gqd", rounded, keys[:, :DL], preferred_element_type=jnp.float32)
    return top, total, summed


def split3(x):
    hi = lax.reduce_precision(x, exponent_bits=8, mantissa_bits=7)
    rest = x - hi
    mid = lax.reduce_precision(rest, exponent_bits=8, mantissa_bits=7)
    lo = lax.reduce_precision(rest - mid, exponent_bits=8, mantissa_bits=7)
    return [hi.astype(jnp.bfloat16), mid.astype(jnp.bfloat16), lo.astype(jnp.bfloat16)]


def own_partial(queries, keys, valid):
    scores = jnp.einsum("shk,tk->sht", queries, keys, preferred_element_type=jnp.float32) * score_scale
    scores = jnp.where(valid, scores, neg_large)
    top = jnp.max(scores, axis=-1)
    weights = jnp.where(valid, jnp.exp(scores - top[..., None]), 0.0)
    total = jnp.sum(weights, axis=-1)
    summed = jnp.einsum(
        "sht,td->shd", weights.astype(jnp.bfloat16), keys[:, :DL], preferred_element_type=jnp.float32
    )
    return top, total, summed


def on_device(queries, prompt_cache, suffix_cache, new_latent, suffix_len, parent, fork_pages):
    steps_n, _, head_dev, width = queries.shape
    pages_n, page_len = suffix_cache.shape[1], suffix_cache.shape[2]
    suffix_n = pages_n * page_len
    prompt_n = prompt_cache.shape[0]
    chips = lax.axis_size("cx") * lax.axis_size("cy")
    chip = lax.axis_index("cx") * lax.axis_size("cy") + lax.axis_index("cy")
    core = lax.axis_index("core")
    my_beam = chip * 2 + core
    partner_beam = chip * 2 + (1 - core)

    row_n = steps_n * head_dev
    spare = -(-width // LANES) * LANES - width
    lane = lax.broadcasted_iota(jnp.int32, (row_n, spare), 1)
    first = lax.broadcasted_iota(jnp.int32, (row_n, spare), 0) == 0
    meta = jnp.where(lane == 0, parent[0], jnp.where(lane == 1, fork_pages[0, 0], fork_pages[0, 1]))
    meta = jnp.where(first & (lane < 3), meta, 0).astype(jnp.bfloat16)
    packed = jnp.concatenate([queries.reshape(row_n, width), meta], axis=1)
    along_y = lax.all_to_all(
        jnp.broadcast_to(packed[None], (lax.axis_size("cy"),) + packed.shape), "cy", 0, 0, tiled=True
    )
    gathered = lax.all_to_all(
        jnp.broadcast_to(along_y[None], (lax.axis_size("cx"),) + along_y.shape), "cx", 0, 0, tiled=True
    ).reshape((chips,) + packed.shape)
    rows = gathered[:, :, :width]
    meta_all = gathered[:, 0, width : width + 3].astype(jnp.int32)
    par, fp0, fp1 = meta_all[:, 0], meta_all[:, 1], meta_all[:, 2]

    own_suffix = suffix_cache.reshape(suffix_n, width)
    local_keys = jnp.concatenate([prompt_cache, own_suffix], axis=0)
    partner_keys, partner_len = lax.ppermute((local_keys, suffix_len), "core", [(0, 1), (1, 0)])
    keys = jnp.concatenate([local_keys, partner_keys], axis=0)

    position = jnp.arange(suffix_n, dtype=jnp.int32)
    page = position // page_len

    def fork_count(owner, length):
        hits = (page[None, :] == fp0[:, None]).astype(jnp.float32) + (page[None, :] == fp1[:, None]).astype(
            jnp.float32
        )
        keep = (par == owner)[:, None] & (position < length)[None, :]
        return jnp.where(keep, hits, 0.0)

    ones = jnp.ones((chips, prompt_n), jnp.float32)
    mult = jnp.concatenate(
        [ones, fork_count(my_beam, suffix_len[0]), ones, fork_count(partner_beam, partner_len[0])], axis=1
    )
    top, total, summed = masked_softmax(rows, keys, mult)
    out = (summed / total[..., None]).astype(jnp.bfloat16)

    out_rows = out.reshape(chips, -1, LANES)
    parts = jnp.stack(split3(top) + split3(total), axis=1).reshape(chips, -1)
    stat_rows = -(-parts.shape[1] // (META_ROWS * LANES)) * META_ROWS
    parts = jnp.pad(parts, ((0, 0), (0, stat_rows * LANES - parts.shape[1])))
    payload = jnp.concatenate([out_rows, parts.reshape(chips, stat_rows, LANES)], axis=1)
    arrived = lax.all_to_all(payload, ("cx", "cy"), 0, 0, tiled=True)
    n_out = out_rows.shape[1]
    out_r = arrived[:, :n_out].reshape(chips, row_n, DL)
    got = arrived[:, n_out:].reshape(chips, -1)[:, : 6 * row_n].astype(jnp.float32).reshape(chips, 6, row_n)
    top_r = (got[:, 0] + got[:, 1]) + got[:, 2]
    total_r = (got[:, 3] + got[:, 4]) + got[:, 5]

    own_keys = jnp.concatenate([own_suffix, new_latent[:, 0, :]], axis=0)
    old_valid = jnp.broadcast_to((position < suffix_len[0])[None, :], (steps_n, suffix_n))
    new_valid = jnp.arange(steps_n, dtype=jnp.int32)[None, :] <= jnp.arange(steps_n, dtype=jnp.int32)[:, None]
    own_valid = jnp.concatenate([old_valid, new_valid], axis=1)[:, None, :]
    top_l, total_l, summed_l = own_partial(queries[:, 0], own_keys, own_valid)

    top_l = top_l.reshape(row_n)
    total_l = total_l.reshape(row_n)
    summed_l = summed_l.reshape(row_n, DL)
    peak = jnp.maximum(jnp.max(top_r, axis=0), top_l)
    weight_r = total_r * jnp.exp(top_r - peak[None])
    weight_l = jnp.exp(top_l - peak)
    denom = jnp.sum(weight_r, axis=0) + total_l * weight_l
    numer = jnp.sum(weight_r[..., None] * out_r.astype(jnp.float32), axis=0) + weight_l[:, None] * summed_l
    result = (numer / denom[:, None]).astype(jnp.bfloat16)
    return result.reshape(steps_n, 1, head_dev, DL)


def chip_grid(devices):
    try:
        xs = {d.coords[0] for d in devices.flat}
        ys = {d.coords[1] for d in devices.flat}
        if len(xs) * len(ys) * 2 == devices.shape[0]:
            return len(xs), len(ys)
    except (AttributeError, IndexError, TypeError):
        pass
    return 1, devices.shape[0] // 2


def solution(mesh):
    req_n, head_n = mesh.devices.shape
    x_n, y_n = chip_grid(mesh.devices)
    devices = mesh.devices.reshape(x_n, y_n, 2, head_n)
    split = Mesh(devices, ("cx", "cy", "core", "hd"))
    beam = ("cx", "cy", "core")
    placed = (
        P(None, beam, "hd", None),
        P(beam, None),
        P(beam, None, None, None),
        P(None, beam, None),
        P(beam),
        P(beam),
        P(beam, None),
    )
    return jax.shard_map(
        on_device,
        mesh=split,
        in_specs=placed,
        out_specs=P(None, beam, "hd", None),
        check_vma=False,
    )
```

```python
import jax
import jax.numpy as jnp
from jax import lax
from jax.sharding import Mesh
from jax.sharding import PartitionSpec as P

DL = 512
LANES = 128
META_ROWS = 16

score_scale = 192.0 ** (-0.5)
neg_large = -1e30


def prompt_softmax(rows, keys):
    scores = jnp.einsum("gqk,tk->gqt", rows, keys, preferred_element_type=jnp.float32) * score_scale
    top = jnp.max(scores, axis=-1)
    weights = jnp.exp(scores - top[..., None])
    total = jnp.sum(weights, axis=-1)
    summed = jnp.einsum(
        "gqt,td->gqd", weights.astype(jnp.bfloat16), keys[:, :DL], preferred_element_type=jnp.float32
    )
    return top, total, summed


def fork_softmax(rows, keys, valid):
    scores = jnp.einsum("gqk,gtk->gqt", rows, keys, preferred_element_type=jnp.float32) * score_scale
    v = valid[:, None, :]
    top = jnp.max(jnp.where(v, scores, neg_large), axis=-1)
    weights = jnp.where(v, jnp.exp(scores - top[..., None]), 0.0)
    total = jnp.sum(weights, axis=-1)
    summed = jnp.einsum(
        "gqt,gtd->gqd", weights.astype(jnp.bfloat16), keys[..., :DL], preferred_element_type=jnp.float32
    )
    return top, total, summed


def masked_softmax(rows, keys, mult):
    scores = jnp.einsum("gqk,tk->gqt", rows, keys, preferred_element_type=jnp.float32) * score_scale
    m = mult[:, None, :]
    valid = m > 0
    top = jnp.max(jnp.where(valid, scores, neg_large), axis=-1)
    weights = jnp.where(valid, jnp.exp(scores - top[..., None]), 0.0)
    total = jnp.sum(weights * m, axis=-1)
    rounded = weights.astype(jnp.bfloat16) * m.astype(jnp.bfloat16)
    summed = jnp.einsum("gqt,td->gqd", rounded, keys[:, :DL], preferred_element_type=jnp.float32)
    return top, total, summed


def split3(x):
    hi = lax.reduce_precision(x, exponent_bits=8, mantissa_bits=7)
    rest = x - hi
    mid = lax.reduce_precision(rest, exponent_bits=8, mantissa_bits=7)
    lo = lax.reduce_precision(rest - mid, exponent_bits=8, mantissa_bits=7)
    return [hi.astype(jnp.bfloat16), mid.astype(jnp.bfloat16), lo.astype(jnp.bfloat16)]


def own_partial(queries, keys, valid):
    scores = jnp.einsum("shk,tk->sht", queries, keys, preferred_element_type=jnp.float32) * score_scale
    scores = jnp.where(valid, scores, neg_large)
    top = jnp.max(scores, axis=-1)
    weights = jnp.where(valid, jnp.exp(scores - top[..., None]), 0.0)
    total = jnp.sum(weights, axis=-1)
    summed = jnp.einsum(
        "sht,td->shd", weights.astype(jnp.bfloat16), keys[:, :DL], preferred_element_type=jnp.float32
    )
    return top, total, summed


def on_device(queries, prompt_cache, suffix_cache, new_latent, suffix_len, parent, fork_pages):
    steps_n, _, head_dev, width = queries.shape
    pages_n, page_len = suffix_cache.shape[1], suffix_cache.shape[2]
    suffix_n = pages_n * page_len
    prompt_n = prompt_cache.shape[0]
    chips = lax.axis_size("cx") * lax.axis_size("cy")
    chip = lax.axis_index("cx") * lax.axis_size("cy") + lax.axis_index("cy")
    core = lax.axis_index("core")
    my_beam = chip * 2 + core
    partner_beam = chip * 2 + (1 - core)

    q_rows = steps_n * head_dev * width // LANES
    lane = lax.broadcasted_iota(jnp.int32, (META_ROWS, LANES), 1)
    first = lax.broadcasted_iota(jnp.int32, (META_ROWS, LANES), 0) == 0
    meta = jnp.where(lane == 0, parent[0], jnp.where(lane == 1, fork_pages[0, 0], fork_pages[0, 1]))
    meta = jnp.where(first & (lane < 3), meta, 0).astype(jnp.bfloat16)
    packed = jnp.concatenate([queries.reshape(q_rows, LANES), meta], axis=0)
    along_y = lax.all_to_all(
        jnp.broadcast_to(packed[None], (lax.axis_size("cy"),) + packed.shape), "cy", 0, 0, tiled=True
    )
    gathered = lax.all_to_all(
        jnp.broadcast_to(along_y[None], (lax.axis_size("cx"),) + along_y.shape), "cx", 0, 0, tiled=True
    ).reshape((chips,) + packed.shape)
    rows = gathered[:, :q_rows].reshape(chips, steps_n * head_dev, width)
    meta_all = gathered[:, q_rows, :3].astype(jnp.int32)
    par, fp0, fp1 = meta_all[:, 0], meta_all[:, 1], meta_all[:, 2]

    own_suffix = suffix_cache.reshape(suffix_n, width)
    local_keys = jnp.concatenate([prompt_cache, own_suffix], axis=0)
    partner_keys, partner_len = lax.ppermute((local_keys, suffix_len), "core", [(0, 1), (1, 0)])
    prompt_keys = jnp.concatenate([prompt_cache, partner_keys[:prompt_n]], axis=0)
    pages = jnp.concatenate(
        [suffix_cache[0], partner_keys[prompt_n:].reshape(pages_n, page_len, width)], axis=0
    )

    mine = par == my_beam
    here = mine | (par == partner_beam)
    picked = jnp.stack([fp0, fp1], axis=1)
    fork_keys = pages[jnp.where(mine, 0, pages_n)[:, None] + picked].reshape(chips, -1, width)
    length = jnp.where(mine, suffix_len[0], partner_len[0])
    offsets = (picked[:, :, None] * page_len + jnp.arange(page_len, dtype=jnp.int32)[None, None, :]).reshape(chips, -1)
    fork_ok = here[:, None] & (offsets < length[:, None])

    top_p, total_p, summed_p = prompt_softmax(rows, prompt_keys)
    top_f, total_f, summed_f = fork_softmax(rows, fork_keys, fork_ok)
    top = jnp.maximum(top_p, top_f)
    scale_p = jnp.exp(top_p - top)
    scale_f = jnp.exp(top_f - top)
    total = scale_p * total_p + scale_f * total_f
    out = ((scale_p[..., None] * summed_p + scale_f[..., None] * summed_f) / total[..., None]).astype(jnp.bfloat16)

    out_rows = out.reshape(chips, -1, LANES)
    parts = jnp.stack(split3(top) + split3(total), axis=1).reshape(chips, -1)
    stat_rows = -(-parts.shape[1] // (META_ROWS * LANES)) * META_ROWS
    parts = jnp.pad(parts, ((0, 0), (0, stat_rows * LANES - parts.shape[1])))
    payload = jnp.concatenate([out_rows, parts.reshape(chips, stat_rows, LANES)], axis=1)
    arrived = lax.all_to_all(payload, ("cx", "cy"), 0, 0, tiled=True)
    n_out = out_rows.shape[1]
    row_n = steps_n * head_dev
    out_r = arrived[:, :n_out].reshape(chips, row_n, DL)
    got = arrived[:, n_out:].reshape(chips, -1)[:, : 6 * row_n].astype(jnp.float32).reshape(chips, 6, row_n)
    top_r = (got[:, 0] + got[:, 1]) + got[:, 2]
    total_r = (got[:, 3] + got[:, 4]) + got[:, 5]

    position = jnp.arange(suffix_n, dtype=jnp.int32)
    own_keys = jnp.concatenate([own_suffix, new_latent[:, 0, :]], axis=0)
    old_valid = jnp.broadcast_to((position < suffix_len[0])[None, :], (steps_n, suffix_n))
    new_valid = jnp.arange(steps_n, dtype=jnp.int32)[None, :] <= jnp.arange(steps_n, dtype=jnp.int32)[:, None]
    own_valid = jnp.concatenate([old_valid, new_valid], axis=1)[:, None, :]
    top_l, total_l, summed_l = own_partial(queries[:, 0], own_keys, own_valid)

    top_l = top_l.reshape(row_n)
    total_l = total_l.reshape(row_n)
    summed_l = summed_l.reshape(row_n, DL)
    peak = jnp.maximum(jnp.max(top_r, axis=0), top_l)
    weight_r = total_r * jnp.exp(top_r - peak[None])
    weight_l = jnp.exp(top_l - peak)
    denom = jnp.sum(weight_r, axis=0) + total_l * weight_l
    numer = jnp.sum(weight_r[..., None] * out_r.astype(jnp.float32), axis=0) + weight_l[:, None] * summed_l
    result = (numer / denom[:, None]).astype(jnp.bfloat16)
    return result.reshape(steps_n, 1, head_dev, DL)


def chip_grid(devices):
    try:
        xs = {d.coords[0] for d in devices.flat}
        ys = {d.coords[1] for d in devices.flat}
        if len(xs) * len(ys) * 2 == devices.shape[0]:
            return len(xs), len(ys)
    except (AttributeError, IndexError, TypeError):
        pass
    return 1, devices.shape[0] // 2


def solution(mesh):
    req_n, head_n = mesh.devices.shape
    x_n, y_n = chip_grid(mesh.devices)
    devices = mesh.devices.reshape(x_n, y_n, 2, head_n)
    split = Mesh(devices, ("cx", "cy", "core", "hd"))
    beam = ("cx", "cy", "core")
    placed = (
        P(None, beam, "hd", None),
        P(beam, None),
        P(beam, None, None, None),
        P(None, beam, None),
        P(beam),
        P(beam),
        P(beam, None),
    )
    return jax.shard_map(
        on_device,
        mesh=split,
        in_specs=placed,
        out_specs=P(None, beam, "hd", None),
        check_vma=False,
    )
```

```python
import jax
import jax.numpy as jnp
from jax import lax
from jax.sharding import Mesh
from jax.sharding import PartitionSpec as P

DL = 512
LANES = 128
META_ROWS = 16

score_scale = 192.0 ** (-0.5)
neg_large = -1e30


def masked_softmax(rows, keys, mult):
    scores = jnp.einsum("gqk,tk->gqt", rows, keys, preferred_element_type=jnp.float32) * score_scale
    m = mult[:, None, :]
    valid = m > 0
    top = jnp.max(jnp.where(valid, scores, neg_large), axis=-1)
    weights = jnp.where(valid, jnp.exp(scores - top[..., None]), 0.0)
    total = jnp.sum(weights * m, axis=-1)
    rounded = weights.astype(jnp.bfloat16) * m.astype(jnp.bfloat16)
    summed = jnp.einsum("gqt,td->gqd", rounded, keys[:, :DL], preferred_element_type=jnp.float32)
    return top, total, summed


def split3(x):
    hi = lax.reduce_precision(x, exponent_bits=8, mantissa_bits=7)
    rest = x - hi
    mid = lax.reduce_precision(rest, exponent_bits=8, mantissa_bits=7)
    lo = lax.reduce_precision(rest - mid, exponent_bits=8, mantissa_bits=7)
    return [hi.astype(jnp.bfloat16), mid.astype(jnp.bfloat16), lo.astype(jnp.bfloat16)]


def own_partial(queries, keys, valid):
    scores = jnp.einsum("shk,tk->sht", queries, keys, preferred_element_type=jnp.float32) * score_scale
    scores = jnp.where(valid, scores, neg_large)
    top = jnp.max(scores, axis=-1)
    weights = jnp.where(valid, jnp.exp(scores - top[..., None]), 0.0)
    total = jnp.sum(weights, axis=-1)
    summed = jnp.einsum(
        "sht,td->shd", weights.astype(jnp.bfloat16), keys[:, :DL], preferred_element_type=jnp.float32
    )
    return top, total, summed


def on_device(queries, prompt_cache, suffix_cache, new_latent, suffix_len, parent, fork_pages):
    steps_n, _, head_dev, width = queries.shape
    pages_n, page_len = suffix_cache.shape[1], suffix_cache.shape[2]
    suffix_n = pages_n * page_len
    prompt_n = prompt_cache.shape[0]
    chips = lax.axis_size("cx") * lax.axis_size("cy")
    chip = lax.axis_index("cx") * lax.axis_size("cy") + lax.axis_index("cy")
    core = lax.axis_index("core")
    my_beam = chip * 2 + core
    partner_beam = chip * 2 + (1 - core)

    q_rows = steps_n * head_dev * width // LANES
    lane = lax.broadcasted_iota(jnp.int32, (META_ROWS, LANES), 1)
    first = lax.broadcasted_iota(jnp.int32, (META_ROWS, LANES), 0) == 0
    meta = jnp.where(lane == 0, parent[0], jnp.where(lane == 1, fork_pages[0, 0], fork_pages[0, 1]))
    meta = jnp.where(first & (lane < 3), meta, 0).astype(jnp.bfloat16)
    packed = jnp.concatenate([queries.reshape(q_rows, LANES), meta], axis=0)
    x_n, y_n = lax.axis_size("cx"), lax.axis_size("cy")
    x_me = lax.axis_index("cx")
    along_y = lax.all_to_all(jnp.broadcast_to(packed[None], (y_n,) + packed.shape), "cy", 0, 0, tiled=True)
    along_x = lax.all_to_all(jnp.broadcast_to(along_y[None], (x_n,) + along_y.shape), "cx", 0, 0, tiled=True)
    others = (x_me + 1 + jnp.arange(x_n - 1, dtype=jnp.int32)) % x_n
    far = jnp.take(along_x, others, axis=0).reshape(((x_n - 1) * y_n,) + packed.shape)

    own_suffix = suffix_cache.reshape(suffix_n, width)
    local_keys = jnp.concatenate([prompt_cache, own_suffix], axis=0)
    partner_keys, partner_len = lax.ppermute((local_keys, suffix_len), "core", [(0, 1), (1, 0)])
    keys = jnp.concatenate([local_keys, partner_keys], axis=0)

    position = jnp.arange(suffix_n, dtype=jnp.int32)
    page = position // page_len
    ones = jnp.ones((prompt_n,), jnp.float32)

    def partials(block):
        n = block.shape[0]
        rows = block[:, :q_rows].reshape(n, steps_n * head_dev, width)
        meta_all = block[:, q_rows, :3].astype(jnp.int32)
        par, fp0, fp1 = meta_all[:, 0], meta_all[:, 1], meta_all[:, 2]

        def fork_count(owner, length):
            hits = (page[None, :] == fp0[:, None]).astype(jnp.float32) + (
                page[None, :] == fp1[:, None]
            ).astype(jnp.float32)
            keep = (par == owner)[:, None] & (position < length)[None, :]
            return jnp.where(keep, hits, 0.0)

        full = jnp.broadcast_to(ones[None], (n, prompt_n))
        mult = jnp.concatenate(
            [full, fork_count(my_beam, suffix_len[0]), full, fork_count(partner_beam, partner_len[0])], axis=1
        )
        top, total, summed = masked_softmax(rows, keys, mult)
        return (summed / total[..., None]).astype(jnp.bfloat16), top, total

    near_out, near_top, near_total = partials(along_y)
    far_out, far_top, far_total = partials(far)
    out = jnp.concatenate([near_out, far_out], axis=0)
    top = jnp.concatenate([near_top, far_top], axis=0)
    total = jnp.concatenate([near_total, far_total], axis=0)

    out_rows = out.reshape(chips, -1, LANES)
    parts = jnp.stack(split3(top) + split3(total), axis=1).reshape(chips, -1)
    stat_rows = -(-parts.shape[1] // (META_ROWS * LANES)) * META_ROWS
    parts = jnp.pad(parts, ((0, 0), (0, stat_rows * LANES - parts.shape[1])))
    payload = jnp.concatenate([out_rows, parts.reshape(chips, stat_rows, LANES)], axis=1)
    unroll = (jnp.arange(x_n, dtype=jnp.int32) - x_me) % x_n
    payload = jnp.take(payload.reshape((x_n, y_n) + payload.shape[1:]), unroll, axis=0).reshape(payload.shape)
    arrived = lax.all_to_all(payload, ("cx", "cy"), 0, 0, tiled=True)
    n_out = out_rows.shape[1]
    row_n = steps_n * head_dev
    out_r = arrived[:, :n_out].reshape(chips, row_n, DL)
    got = arrived[:, n_out:].reshape(chips, -1)[:, : 6 * row_n].astype(jnp.float32).reshape(chips, 6, row_n)
    top_r = (got[:, 0] + got[:, 1]) + got[:, 2]
    total_r = (got[:, 3] + got[:, 4]) + got[:, 5]

    own_keys = jnp.concatenate([own_suffix, new_latent[:, 0, :]], axis=0)
    old_valid = jnp.broadcast_to((position < suffix_len[0])[None, :], (steps_n, suffix_n))
    new_valid = jnp.arange(steps_n, dtype=jnp.int32)[None, :] <= jnp.arange(steps_n, dtype=jnp.int32)[:, None]
    own_valid = jnp.concatenate([old_valid, new_valid], axis=1)[:, None, :]
    top_l, total_l, summed_l = own_partial(queries[:, 0], own_keys, own_valid)

    top_l = top_l.reshape(row_n)
    total_l = total_l.reshape(row_n)
    summed_l = summed_l.reshape(row_n, DL)
    peak = jnp.maximum(jnp.max(top_r, axis=0), top_l)
    weight_r = total_r * jnp.exp(top_r - peak[None])
    weight_l = jnp.exp(top_l - peak)
    denom = jnp.sum(weight_r, axis=0) + total_l * weight_l
    numer = jnp.sum(weight_r[..., None] * out_r.astype(jnp.float32), axis=0) + weight_l[:, None] * summed_l
    result = (numer / denom[:, None]).astype(jnp.bfloat16)
    return result.reshape(steps_n, 1, head_dev, DL)


def chip_grid(devices):
    try:
        xs = {d.coords[0] for d in devices.flat}
        ys = {d.coords[1] for d in devices.flat}
        if len(xs) * len(ys) * 2 == devices.shape[0]:
            return len(xs), len(ys)
    except (AttributeError, IndexError, TypeError):
        pass
    return 1, devices.shape[0] // 2


def solution(mesh):
    req_n, head_n = mesh.devices.shape
    x_n, y_n = chip_grid(mesh.devices)
    devices = mesh.devices.reshape(x_n, y_n, 2, head_n)
    split = Mesh(devices, ("cx", "cy", "core", "hd"))
    beam = ("cx", "cy", "core")
    placed = (
        P(None, beam, "hd", None),
        P(beam, None),
        P(beam, None, None, None),
        P(None, beam, None),
        P(beam),
        P(beam),
        P(beam, None),
    )
    return jax.shard_map(
        on_device,
        mesh=split,
        in_specs=placed,
        out_specs=P(None, beam, "hd", None),
        check_vma=False,
    )
```

```python
import jax
import jax.numpy as jnp
from jax import lax
from jax.sharding import Mesh
from jax.sharding import PartitionSpec as P

DL = 512
LANES = 128
META_ROWS = 16

score_scale = 192.0 ** (-0.5)
neg_large = -1e30


def masked_softmax(rows, keys, mult):
    scores = jnp.einsum("gqk,tk->gqt", rows, keys, preferred_element_type=jnp.float32) * score_scale
    m = mult[:, None, :]
    valid = m > 0
    top = jnp.max(jnp.where(valid, scores, neg_large), axis=-1)
    weights = jnp.where(valid, jnp.exp(scores - top[..., None]), 0.0)
    total = jnp.sum(weights * m, axis=-1)
    rounded = weights.astype(jnp.bfloat16) * m.astype(jnp.bfloat16)
    summed = jnp.einsum("gqt,td->gqd", rounded, keys[:, :DL], preferred_element_type=jnp.float32)
    return top, total, summed


def split3(x):
    hi = lax.reduce_precision(x, exponent_bits=8, mantissa_bits=7)
    rest = x - hi
    mid = lax.reduce_precision(rest, exponent_bits=8, mantissa_bits=7)
    lo = lax.reduce_precision(rest - mid, exponent_bits=8, mantissa_bits=7)
    return [hi.astype(jnp.bfloat16), mid.astype(jnp.bfloat16), lo.astype(jnp.bfloat16)]


def own_partial(queries, keys, valid):
    scores = jnp.einsum("shk,tk->sht", queries, keys, preferred_element_type=jnp.float32) * score_scale
    scores = jnp.where(valid, scores, neg_large)
    top = jnp.max(scores, axis=-1)
    weights = jnp.where(valid, jnp.exp(scores - top[..., None]), 0.0)
    total = jnp.sum(weights, axis=-1)
    summed = jnp.einsum(
        "sht,td->shd", weights.astype(jnp.bfloat16), keys[:, :DL], preferred_element_type=jnp.float32
    )
    return top, total, summed


def on_device(queries, prompt_cache, suffix_cache, new_latent, suffix_len, parent, fork_pages):
    steps_n, _, head_dev, width = queries.shape
    pages_n, page_len = suffix_cache.shape[1], suffix_cache.shape[2]
    suffix_n = pages_n * page_len
    prompt_n = prompt_cache.shape[0]
    chips = lax.axis_size("cx") * lax.axis_size("cy")
    chip = lax.axis_index("cx") * lax.axis_size("cy") + lax.axis_index("cy")
    core = lax.axis_index("core")
    my_beam = chip * 2 + core
    partner_beam = chip * 2 + (1 - core)

    q_rows = steps_n * head_dev * width // LANES
    meta = jnp.concatenate([parent, fork_pages.reshape(-1)]).astype(jnp.bfloat16)
    meta = jnp.pad(meta, (0, META_ROWS * LANES - meta.shape[0])).reshape(META_ROWS, LANES)
    packed = jnp.concatenate([queries.reshape(q_rows, LANES), meta], axis=0)
    along_y = lax.all_to_all(
        jnp.broadcast_to(packed[None], (lax.axis_size("cy"),) + packed.shape), "cy", 0, 0, tiled=True
    )
    gathered = lax.all_to_all(
        jnp.broadcast_to(along_y[None], (lax.axis_size("cx"),) + along_y.shape), "cx", 0, 0, tiled=True
    ).reshape((chips,) + packed.shape)
    rows = gathered[:, :q_rows].reshape(chips, steps_n * head_dev, width)
    meta_all = gathered[:, q_rows, :3].astype(jnp.int32)
    par, fp0, fp1 = meta_all[:, 0], meta_all[:, 1], meta_all[:, 2]

    own_suffix = suffix_cache.reshape(suffix_n, width)
    local_keys = jnp.concatenate([prompt_cache, own_suffix], axis=0)
    partner_keys, partner_len = lax.ppermute((local_keys, suffix_len), "core", [(0, 1), (1, 0)])
    keys = jnp.concatenate([local_keys, partner_keys], axis=0)

    position = jnp.arange(suffix_n, dtype=jnp.int32)
    page = position // page_len

    def fork_count(owner, length):
        hits = (page[None, :] == fp0[:, None]).astype(jnp.float32) + (page[None, :] == fp1[:, None]).astype(
            jnp.float32
        )
        keep = (par == owner)[:, None] & (position < length)[None, :]
        return jnp.where(keep, hits, 0.0)

    ones = jnp.ones((chips, prompt_n), jnp.float32)
    mult = jnp.concatenate(
        [ones, fork_count(my_beam, suffix_len[0]), ones, fork_count(partner_beam, partner_len[0])], axis=1
    )
    top, total, summed = masked_softmax(rows, keys, mult)
    out = (summed / total[..., None]).astype(jnp.bfloat16)

    out_rows = out.reshape(chips, -1, LANES)
    parts = jnp.stack(split3(top) + split3(total), axis=1).reshape(chips, -1)
    stat_rows = -(-parts.shape[1] // (META_ROWS * LANES)) * META_ROWS
    parts = jnp.pad(parts, ((0, 0), (0, stat_rows * LANES - parts.shape[1])))
    payload = jnp.concatenate([out_rows, parts.reshape(chips, stat_rows, LANES)], axis=1)
    arrived = lax.all_to_all(payload, ("cx", "cy"), 0, 0, tiled=True)
    n_out = out_rows.shape[1]
    row_n = steps_n * head_dev
    out_r = arrived[:, :n_out].reshape(chips, row_n, DL)
    got = arrived[:, n_out:].reshape(chips, -1)[:, : 6 * row_n].astype(jnp.float32).reshape(chips, 6, row_n)
    top_r = (got[:, 0] + got[:, 1]) + got[:, 2]
    total_r = (got[:, 3] + got[:, 4]) + got[:, 5]

    own_keys = jnp.concatenate([own_suffix, new_latent[:, 0, :]], axis=0)
    old_valid = jnp.broadcast_to((position < suffix_len[0])[None, :], (steps_n, suffix_n))
    new_valid = jnp.arange(steps_n, dtype=jnp.int32)[None, :] <= jnp.arange(steps_n, dtype=jnp.int32)[:, None]
    own_valid = jnp.concatenate([old_valid, new_valid], axis=1)[:, None, :]
    top_l, total_l, summed_l = own_partial(queries[:, 0], own_keys, own_valid)

    top_l = top_l.reshape(row_n)
    total_l = total_l.reshape(row_n)
    summed_l = summed_l.reshape(row_n, DL)
    peak = jnp.maximum(jnp.max(top_r, axis=0), top_l)
    weight_r = total_r * jnp.exp(top_r - peak[None])
    weight_l = jnp.exp(top_l - peak)
    denom = jnp.sum(weight_r, axis=0) + total_l * weight_l
    numer = jnp.sum(weight_r[..., None] * out_r.astype(jnp.float32), axis=0) + weight_l[:, None] * summed_l
    result = (numer / denom[:, None]).astype(jnp.bfloat16)
    return result.reshape(steps_n, 1, head_dev, DL)


def chip_grid(devices):
    try:
        xs = {d.coords[0] for d in devices.flat}
        ys = {d.coords[1] for d in devices.flat}
        if len(xs) * len(ys) * 2 == devices.shape[0]:
            return len(xs), len(ys)
    except (AttributeError, IndexError, TypeError):
        pass
    return 1, devices.shape[0] // 2


def solution(mesh):
    req_n, head_n = mesh.devices.shape
    x_n, y_n = chip_grid(mesh.devices)
    devices = mesh.devices.reshape(x_n, y_n, 2, head_n)
    split = Mesh(devices, ("cx", "cy", "core", "hd"))
    beam = ("cx", "cy", "core")
    placed = (
        P(None, beam, "hd", None),
        P(beam, None),
        P(beam, None, None, None),
        P(None, beam, None),
        P(beam),
        P(beam),
        P(beam, None),
    )
    return jax.shard_map(
        on_device,
        mesh=split,
        in_specs=placed,
        out_specs=P(None, beam, "hd", None),
        check_vma=False,
    )
```

```python
import jax
import jax.numpy as jnp
from jax import lax
from jax.sharding import Mesh
from jax.sharding import PartitionSpec as P

DL = 512
LANES = 128
META_ROWS = 16

score_scale = 192.0 ** (-0.5)
neg_large = -1e30


def masked_softmax(rows, keys, mult):
    scores = jnp.einsum("gqk,tk->gqt", rows, keys, preferred_element_type=jnp.float32) * score_scale
    m = mult[:, None, :]
    valid = m > 0
    top = jnp.max(jnp.where(valid, scores, neg_large), axis=-1)
    weights = jnp.where(valid, jnp.exp(scores - top[..., None]), 0.0)
    total = jnp.sum(weights * m, axis=-1)
    rounded = weights.astype(jnp.bfloat16) * m.astype(jnp.bfloat16)
    summed = jnp.einsum("gqt,td->gqd", rounded, keys[:, :DL], preferred_element_type=jnp.float32)
    return top, total, summed


def split3(x):
    hi = lax.reduce_precision(x, exponent_bits=8, mantissa_bits=7)
    rest = x - hi
    mid = lax.reduce_precision(rest, exponent_bits=8, mantissa_bits=7)
    lo = lax.reduce_precision(rest - mid, exponent_bits=8, mantissa_bits=7)
    return [hi.astype(jnp.bfloat16), mid.astype(jnp.bfloat16), lo.astype(jnp.bfloat16)]


def own_partial(queries, keys, valid):
    scores = jnp.einsum("shk,tk->sht", queries, keys, preferred_element_type=jnp.float32) * score_scale
    scores = jnp.where(valid, scores, neg_large)
    top = jnp.max(scores, axis=-1)
    weights = jnp.where(valid, jnp.exp(scores - top[..., None]), 0.0)
    total = jnp.sum(weights, axis=-1)
    summed = jnp.einsum(
        "sht,td->shd", weights.astype(jnp.bfloat16), keys[:, :DL], preferred_element_type=jnp.float32
    )
    return top, total, summed


def on_device(queries, prompt_cache, suffix_cache, new_latent, suffix_len, parent, fork_pages):
    steps_n, _, head_dev, width = queries.shape
    pages_n, page_len = suffix_cache.shape[1], suffix_cache.shape[2]
    suffix_n = pages_n * page_len
    prompt_n = prompt_cache.shape[0]
    chips = lax.axis_size("cx") * lax.axis_size("cy")
    chip = lax.axis_index("cx") * lax.axis_size("cy") + lax.axis_index("cy")
    core = lax.axis_index("core")
    my_beam = chip * 2 + core
    partner_beam = chip * 2 + (1 - core)

    q_rows = steps_n * head_dev * width // LANES
    meta = jnp.concatenate([parent, fork_pages.reshape(-1)]).astype(jnp.bfloat16)
    meta = jnp.pad(meta, (0, META_ROWS * LANES - meta.shape[0])).reshape(META_ROWS, LANES)
    packed = jnp.concatenate([queries.reshape(q_rows, LANES), meta], axis=0)
    along_y = lax.all_to_all(
        jnp.broadcast_to(packed[None], (lax.axis_size("cy"),) + packed.shape), "cy", 0, 0, tiled=True
    )
    gathered = lax.all_to_all(
        jnp.broadcast_to(along_y[None], (lax.axis_size("cx"),) + along_y.shape), "cx", 0, 0, tiled=True
    ).reshape((chips,) + packed.shape)
    rows = gathered[:, :q_rows].reshape(chips, steps_n * head_dev, width)
    meta_all = gathered[:, q_rows, :3].astype(jnp.int32)
    par, fp0, fp1 = meta_all[:, 0], meta_all[:, 1], meta_all[:, 2]

    own_suffix = suffix_cache.reshape(suffix_n, width)
    local_keys = jnp.concatenate([prompt_cache, own_suffix], axis=0)
    partner_keys, partner_len = lax.ppermute((local_keys, suffix_len), "core", [(0, 1), (1, 0)])
    keys = jnp.concatenate([local_keys, partner_keys], axis=0)

    position = jnp.arange(suffix_n, dtype=jnp.int32)
    page = position // page_len

    def fork_count(owner, length):
        hits = (page[None, :] == fp0[:, None]).astype(jnp.float32) + (page[None, :] == fp1[:, None]).astype(
            jnp.float32
        )
        keep = (par == owner)[:, None] & (position < length)[None, :]
        return jnp.where(keep, hits, 0.0)

    ones = jnp.ones((chips, prompt_n), jnp.float32)
    mult = jnp.concatenate(
        [ones, fork_count(my_beam, suffix_len[0]), ones, fork_count(partner_beam, partner_len[0])], axis=1
    )
    top, total, summed = masked_softmax(rows, keys, mult)
    out = summed.astype(jnp.bfloat16)

    out_rows = out.reshape(chips, -1, LANES)
    parts = jnp.stack(split3(top) + split3(total), axis=1).reshape(chips, -1)
    stat_rows = -(-parts.shape[1] // (META_ROWS * LANES)) * META_ROWS
    parts = jnp.pad(parts, ((0, 0), (0, stat_rows * LANES - parts.shape[1])))
    payload = jnp.concatenate([out_rows, parts.reshape(chips, stat_rows, LANES)], axis=1)
    arrived = lax.all_to_all(payload, ("cx", "cy"), 0, 0, tiled=True)
    n_out = out_rows.shape[1]
    row_n = steps_n * head_dev
    out_r = arrived[:, :n_out].reshape(chips, row_n, DL)
    got = arrived[:, n_out:].reshape(chips, -1)[:, : 6 * row_n].astype(jnp.float32).reshape(chips, 6, row_n)
    top_r = (got[:, 0] + got[:, 1]) + got[:, 2]
    total_r = (got[:, 3] + got[:, 4]) + got[:, 5]

    own_keys = jnp.concatenate([own_suffix, new_latent[:, 0, :]], axis=0)
    old_valid = jnp.broadcast_to((position < suffix_len[0])[None, :], (steps_n, suffix_n))
    new_valid = jnp.arange(steps_n, dtype=jnp.int32)[None, :] <= jnp.arange(steps_n, dtype=jnp.int32)[:, None]
    own_valid = jnp.concatenate([old_valid, new_valid], axis=1)[:, None, :]
    top_l, total_l, summed_l = own_partial(queries[:, 0], own_keys, own_valid)

    top_l = top_l.reshape(row_n)
    total_l = total_l.reshape(row_n)
    summed_l = summed_l.reshape(row_n, DL)
    peak = jnp.maximum(jnp.max(top_r, axis=0), top_l)
    weight_r = jnp.exp(top_r - peak[None])
    weight_l = jnp.exp(top_l - peak)
    denom = jnp.sum(total_r * weight_r, axis=0) + total_l * weight_l
    numer = jnp.sum(weight_r[..., None] * out_r.astype(jnp.float32), axis=0) + weight_l[:, None] * summed_l
    result = (numer / denom[:, None]).astype(jnp.bfloat16)
    return result.reshape(steps_n, 1, head_dev, DL)


def chip_grid(devices):
    try:
        xs = {d.coords[0] for d in devices.flat}
        ys = {d.coords[1] for d in devices.flat}
        if len(xs) * len(ys) * 2 == devices.shape[0]:
            return len(xs), len(ys)
    except (AttributeError, IndexError, TypeError):
        pass
    return 1, devices.shape[0] // 2


def solution(mesh):
    req_n, head_n = mesh.devices.shape
    x_n, y_n = chip_grid(mesh.devices)
    devices = mesh.devices.reshape(x_n, y_n, 2, head_n)
    split = Mesh(devices, ("cx", "cy", "core", "hd"))
    beam = ("cx", "cy", "core")
    placed = (
        P(None, beam, "hd", None),
        P(beam, None),
        P(beam, None, None, None),
        P(None, beam, None),
        P(beam),
        P(beam),
        P(beam, None),
    )
    return jax.shard_map(
        on_device,
        mesh=split,
        in_specs=placed,
        out_specs=P(None, beam, "hd", None),
        check_vma=False,
    )
```

```python
import jax
import jax.numpy as jnp
from jax import lax
from jax.sharding import Mesh
from jax.sharding import PartitionSpec as P

DL = 512
LANES = 128
META_ROWS = 16

score_scale = 192.0 ** (-0.5)
neg_large = -1e30


def masked_softmax(rows, keys, mult):
    scores = jnp.einsum("gqk,tk->gqt", rows, keys, preferred_element_type=jnp.float32) * score_scale
    m = mult[:, None, :]
    valid = m > 0
    top = jnp.max(jnp.where(valid, scores, neg_large), axis=-1)
    weights = jnp.where(valid, jnp.exp(scores - top[..., None]), 0.0)
    total = jnp.sum(weights * m, axis=-1)
    rounded = weights.astype(jnp.bfloat16) * m.astype(jnp.bfloat16)
    summed = jnp.einsum("gqt,td->gqd", rounded, keys[:, :DL], preferred_element_type=jnp.float32)
    return top, total, summed


def split3(x):
    hi = lax.reduce_precision(x, exponent_bits=8, mantissa_bits=7)
    rest = x - hi
    mid = lax.reduce_precision(rest, exponent_bits=8, mantissa_bits=7)
    lo = lax.reduce_precision(rest - mid, exponent_bits=8, mantissa_bits=7)
    return [hi.astype(jnp.bfloat16), mid.astype(jnp.bfloat16), lo.astype(jnp.bfloat16)]


def own_partial(queries, keys, valid):
    scores = jnp.einsum("shk,tk->sht", queries, keys, preferred_element_type=jnp.float32) * score_scale
    scores = jnp.where(valid, scores, neg_large)
    top = jnp.max(scores, axis=-1)
    weights = jnp.where(valid, jnp.exp(scores - top[..., None]), 0.0)
    total = jnp.sum(weights, axis=-1)
    summed = jnp.einsum(
        "sht,td->shd", weights.astype(jnp.bfloat16), keys[:, :DL], preferred_element_type=jnp.float32
    )
    return top, total, summed


def on_device(queries, prompt_cache, suffix_cache, new_latent, suffix_len, parent, fork_pages):
    steps_n, _, head_dev, width = queries.shape
    pages_n, page_len = suffix_cache.shape[1], suffix_cache.shape[2]
    suffix_n = pages_n * page_len
    prompt_n = prompt_cache.shape[0]
    chips = lax.axis_size("cx") * lax.axis_size("cy")
    chip = lax.axis_index("cx") * lax.axis_size("cy") + lax.axis_index("cy")
    core = lax.axis_index("core")
    my_beam = chip * 2 + core
    partner_beam = chip * 2 + (1 - core)

    q_rows = steps_n * head_dev * width // LANES
    meta = jnp.concatenate([parent, fork_pages.reshape(-1)]).astype(jnp.bfloat16)
    meta = jnp.pad(meta, (0, META_ROWS * LANES - meta.shape[0])).reshape(META_ROWS, LANES)
    y_n = lax.axis_size("cy")
    q_flat = queries.reshape(q_rows, LANES)
    send = jnp.concatenate(
        [jnp.broadcast_to(q_flat[None], (y_n,) + q_flat.shape), jnp.broadcast_to(meta[None], (y_n,) + meta.shape)],
        axis=1,
    )
    packed = send[0]
    along_y = lax.all_to_all(send, "cy", 0, 0, tiled=True)
    gathered = lax.all_to_all(
        jnp.broadcast_to(along_y[None], (lax.axis_size("cx"),) + along_y.shape), "cx", 0, 0, tiled=True
    ).reshape((chips,) + packed.shape)
    rows = gathered[:, :q_rows].reshape(chips, steps_n * head_dev, width)
    meta_all = gathered[:, q_rows, :3].astype(jnp.int32)
    par, fp0, fp1 = meta_all[:, 0], meta_all[:, 1], meta_all[:, 2]

    own_suffix = suffix_cache.reshape(suffix_n, width)
    local_keys = jnp.concatenate([prompt_cache, own_suffix], axis=0)
    partner_keys, partner_len = lax.ppermute((local_keys, suffix_len), "core", [(0, 1), (1, 0)])
    keys = jnp.concatenate([local_keys, partner_keys], axis=0)

    position = jnp.arange(suffix_n, dtype=jnp.int32)
    page = position // page_len

    def fork_count(owner, length):
        hits = (page[None, :] == fp0[:, None]).astype(jnp.float32) + (page[None, :] == fp1[:, None]).astype(
            jnp.float32
        )
        keep = (par == owner)[:, None] & (position < length)[None, :]
        return jnp.where(keep, hits, 0.0)

    ones = jnp.ones((chips, prompt_n), jnp.float32)
    mult = jnp.concatenate(
        [ones, fork_count(my_beam, suffix_len[0]), ones, fork_count(partner_beam, partner_len[0])], axis=1
    )
    top, total, summed = masked_softmax(rows, keys, mult)
    out = (summed / total[..., None]).astype(jnp.bfloat16)

    out_rows = out.reshape(chips, -1, LANES)
    parts = jnp.stack(split3(top) + split3(total), axis=1).reshape(chips, -1)
    stat_rows = -(-parts.shape[1] // (META_ROWS * LANES)) * META_ROWS
    parts = jnp.pad(parts, ((0, 0), (0, stat_rows * LANES - parts.shape[1])))
    payload = jnp.concatenate([out_rows, parts.reshape(chips, stat_rows, LANES)], axis=1)
    arrived = lax.all_to_all(payload, ("cx", "cy"), 0, 0, tiled=True)
    n_out = out_rows.shape[1]
    row_n = steps_n * head_dev
    out_r = arrived[:, :n_out].reshape(chips, row_n, DL)
    got = arrived[:, n_out:].reshape(chips, -1)[:, : 6 * row_n].astype(jnp.float32).reshape(chips, 6, row_n)
    top_r = (got[:, 0] + got[:, 1]) + got[:, 2]
    total_r = (got[:, 3] + got[:, 4]) + got[:, 5]

    own_keys = jnp.concatenate([own_suffix, new_latent[:, 0, :]], axis=0)
    old_valid = jnp.broadcast_to((position < suffix_len[0])[None, :], (steps_n, suffix_n))
    new_valid = jnp.arange(steps_n, dtype=jnp.int32)[None, :] <= jnp.arange(steps_n, dtype=jnp.int32)[:, None]
    own_valid = jnp.concatenate([old_valid, new_valid], axis=1)[:, None, :]
    top_l, total_l, summed_l = own_partial(queries[:, 0], own_keys, own_valid)

    top_l = top_l.reshape(row_n)
    total_l = total_l.reshape(row_n)
    summed_l = summed_l.reshape(row_n, DL)
    peak = jnp.maximum(jnp.max(top_r, axis=0), top_l)
    weight_r = total_r * jnp.exp(top_r - peak[None])
    weight_l = jnp.exp(top_l - peak)
    denom = jnp.sum(weight_r, axis=0) + total_l * weight_l
    numer = jnp.sum(weight_r[..., None] * out_r.astype(jnp.float32), axis=0) + weight_l[:, None] * summed_l
    result = (numer / denom[:, None]).astype(jnp.bfloat16)
    return result.reshape(steps_n, 1, head_dev, DL)


def chip_grid(devices):
    try:
        xs = {d.coords[0] for d in devices.flat}
        ys = {d.coords[1] for d in devices.flat}
        if len(xs) * len(ys) * 2 == devices.shape[0]:
            return len(xs), len(ys)
    except (AttributeError, IndexError, TypeError):
        pass
    return 1, devices.shape[0] // 2


def solution(mesh):
    req_n, head_n = mesh.devices.shape
    x_n, y_n = chip_grid(mesh.devices)
    devices = mesh.devices.reshape(x_n, y_n, 2, head_n)
    split = Mesh(devices, ("cx", "cy", "core", "hd"))
    beam = ("cx", "cy", "core")
    placed = (
        P(None, beam, "hd", None),
        P(beam, None),
        P(beam, None, None, None),
        P(None, beam, None),
        P(beam),
        P(beam),
        P(beam, None),
    )
    return jax.shard_map(
        on_device,
        mesh=split,
        in_specs=placed,
        out_specs=P(None, beam, "hd", None),
        check_vma=False,
    )
```
